32 devices in a mesh: seq: 8 (over z, x), kvh: 4 (over y, core).
Axes of the slice: x: 2, y: 2, z: 4, core: 2. Of those that a mesh axis runs over, the one named last changes fastest.
Arguments:
- queries: bfloat16 [2048, 16384], P(('seq', 'kvh')), may hold values from -48 to 48
- key_rows: bfloat16 [2048, 1024], P(('seq', 'kvh')), may hold values from -6 to 6
- value_rows: bfloat16 [2048, 1024], P(('seq', 'kvh')), may hold values from -6 to 6
- doc_lengths: int32 [8], replicated, may hold values from 1 to 512, 2048 in all
Outputs:
- attended: bfloat16 [2048, 16384], P(('seq', 'kvh'))
The draws below stay inside these ranges and needn't reach their ends.
Inputs may be any that keep to these rules, and one draw needn't show every extreme that they name: `doc_lengths`: the lengths add up to 2048; the longest document has exactly 512 tokens.
All inputs are finite; a program needn't handle non-finite values.
Results may differ from the reference program's by a relative error of at most 0.004.
Values may be sent and summed in bfloat16 or wider, within the bound.
No kernel may reach another device: no remote copies, remote signals or barrier semaphores. Data moves between devices by JAX's collectives and lax.ppermute only.
A program may use at most 64 MiB of HBM per device.

```python
import math
import jax
import jax.numpy as jnp
import numpy as np
from jax import lax

DH = 128
KVH = 8
GROUP = 16
TOK_DEV = 256
CH = 128
NBLOCK = 16
TOKENS = 2048
MOST = 512
NDOCS = 8


def layout_order():
    row_index = jnp.arange(TOKENS, dtype=jnp.int32)
    shard_id = row_index // TOK_DEV
    row_in = row_index % TOK_DEV
    return jnp.where(row_in < CH, shard_id * CH + row_in, (NBLOCK - 1 - shard_id) * CH + row_in - CH)


def shared_draw(key):
    key_seed = jax.random.fold_in(key, 7)
    query_seed = jax.random.fold_in(key, 11)
    place = layout_order()
    key_seq = jnp.clip(jax.random.normal(key_seed, (TOKENS, KVH, DH), jnp.float32), -6.0, 6.0)
    query_seq = jnp.clip(jax.random.normal(query_seed, (TOKENS, KVH, GROUP, DH), jnp.float32), -6.0, 6.0)
    query_out = query_seq.reshape(TOKENS, KVH * GROUP * DH)[place]
    key_out = key_seq.reshape(TOKENS, KVH * DH)[place]
    return (query_out.astype(jnp.bfloat16), key_out.astype(jnp.bfloat16))


def draw_queries(key, part):
    return shared_draw(key)[0]


def draw_key_rows(key, part):
    return shared_draw(key)[1]


def block_scale(rng, shape, split, low, high):
    loudness = 1.0
    for axis_at, blocks in split:
        draws = jax.random.uniform(jax.random.fold_in(jax.random.fold_in(rng, 6), axis_at), (blocks,), jnp.float32, low / len(split), high / len(split))
        loudness = loudness * jnp.repeat(jnp.exp(draws), shape[axis_at] // blocks).reshape((-1,) + (1,) * (len(shape) - 1 - axis_at))
    return loudness


def length_profile(number_of, total, limit, lean):
    weights = [(1 << 20) // math.isqrt(rank ** lean) + 1 for rank in range(2, number_of + 1)]
    spare, counts = total - limit - (number_of - 1), [1] * (number_of - 1)
    while spare > 0:
        movable = [i for i in range(number_of - 1) if counts[i] < limit]
        mass, left = sum([weights[i] for i in movable]), spare
        for i in movable:
            addition = min(limit - counts[i], max(1, left * weights[i] // mass), spare)
            counts[i] = counts[i] + addition
            spare = spare - addition
    return np.array([limit] + counts)


def uneven_parts(key, number_of, total, most, slope):
    if number_of == 2:
        one = jax.random.randint(key, (), max(1, total - most), min(most, total - 1) + 1)
        return jnp.stack([one, total - one])
    tallies = jnp.asarray(length_profile(number_of, total, most, slope), jnp.int32)
    pairs = (number_of - 1) // 2
    source_of, receiver = tallies[1:1 + 2 * pairs:2], tallies[2:2 + 2 * pairs:2]
    room = jnp.minimum(source_of - 1, most - receiver)
    moved = jax.random.randint(jax.random.fold_in(key, 1), (pairs,), 0, 1 << 20) % (room + 1)
    tallies = tallies.at[1:1 + 2 * pairs:2].set(source_of - moved).at[2:2 + 2 * pairs:2].set(receiver + moved)
    return tallies[jax.random.permutation(jax.random.fold_in(key, 2), number_of)]


def bell_draw(own_key, shape, deviation, reach, pieces=(), kind=jnp.bfloat16):
    factor_of = block_scale(own_key, shape, pieces, -0.22, 0.18) if pieces else 1.0
    result = jax.random.normal(own_key, shape, jnp.float32) * deviation * factor_of
    return jnp.minimum(jnp.maximum(result, -reach), reach).astype(kind)


def setup_inputs(seed: int = 0) -> dict:
    key_of = jax.random.split(jax.random.key(seed), 5)
    return {
        "queries": draw_queries(jax.random.fold_in(key_of[4], 71), 0),
        "key_rows": draw_key_rows(jax.random.fold_in(key_of[4], 71), 0),
        "value_rows": bell_draw(key_of[2], (TOKENS, KVH * DH), 1.0, 6.0, ((0, 32),)),
        "doc_lengths": uneven_parts(key_of[3], NDOCS, TOKENS, MOST, 2).astype(jnp.int32),
    }


def layout_position():
    row_index = jnp.arange(TOKENS, dtype=jnp.int32)
    shard_id = row_index // TOK_DEV
    row_in = row_index % TOK_DEV
    return jnp.where(row_in < CH, shard_id * CH + row_in, (NBLOCK - 1 - shard_id) * CH + row_in - CH)

def reference(queries, key_rows, value_rows, doc_lengths):
    position = layout_position()
    inverse = jnp.zeros((TOKENS,), jnp.int32).at[position].set(jnp.arange(TOKENS, dtype=jnp.int32))
    q_seq = queries[inverse].reshape(TOKENS, KVH, GROUP, DH)
    k_seq = key_rows[inverse].reshape(TOKENS, KVH, DH)
    v_seq = value_rows[inverse].reshape(TOKENS, KVH, DH)
    doc_ends = jnp.cumsum(doc_lengths).astype(jnp.int32)
    seq_pos = jnp.arange(TOKENS, dtype=jnp.int32)
    starts = lax.optimization_barrier(jnp.sum(jnp.where(doc_ends[None, :] <= seq_pos[:, None], doc_lengths[None, :], 0), axis=1)).astype(jnp.int32)
    block_rows = min(256, TOKENS)
    margin = (MOST + block_rows - 1) // block_rows * block_rows
    key_span = margin + block_rows
    k_pad = jnp.concatenate([jnp.zeros((margin, KVH, DH), k_seq.dtype), k_seq], axis=0)
    v_pad = jnp.concatenate([jnp.zeros((margin, KVH, DH), v_seq.dtype), v_seq], axis=0)
    pos_pad = jnp.concatenate([jnp.full((margin,), -1, jnp.int32), seq_pos])
    score_scale = 1.0 / math.sqrt(DH)

    def one_block(block_no):
        first_row = (block_no * block_rows).astype(jnp.int32)
        q_block = lax.dynamic_slice_in_dim(q_seq, first_row, block_rows, 0)
        k_block = lax.dynamic_slice_in_dim(k_pad, first_row, key_span, 0)
        v_block = lax.dynamic_slice_in_dim(v_pad, first_row, key_span, 0)
        key_pos = lax.dynamic_slice_in_dim(pos_pad, first_row, key_span, 0)
        query_pos = lax.dynamic_slice_in_dim(seq_pos, first_row, block_rows, 0)
        query_start = lax.dynamic_slice_in_dim(starts, first_row, block_rows, 0)
        allowed = (key_pos[None, :] <= query_pos[:, None]) & (key_pos[None, :] >= query_start[:, None])

        def one_head(head_no):
            q_head = jnp.take(q_block, head_no, axis=1).astype(jnp.float32)
            k_head = jnp.take(k_block, head_no, axis=1).astype(jnp.float32)
            v_head = jnp.take(v_block, head_no, axis=1).astype(jnp.float32)
            scores = jnp.einsum('qgd,kd->gqk', q_head, k_head) * score_scale
            scores = jnp.where(allowed[None], scores, -jnp.inf)
            row_top = lax.optimization_barrier(jnp.max(scores, axis=2, keepdims=True))
            weights = jnp.exp(scores - row_top)
            row_total = lax.optimization_barrier(jnp.sum(weights, axis=2))
            rounded = lax.optimization_barrier(weights.astype(jnp.bfloat16)).astype(jnp.float32)
            mixed = jnp.einsum('gqk,kd->qgd', rounded, v_head)
            return mixed / jnp.transpose(row_total)[:, :, None]
        per_head = lax.map(one_head, jnp.arange(KVH, dtype=jnp.int32))
        return jnp.transpose(per_head, (1, 0, 2, 3)).reshape(block_rows, KVH * GROUP * DH)
    out_seq = lax.map(one_block, jnp.arange(TOKENS // block_rows, dtype=jnp.int32)).reshape(TOKENS, KVH * GROUP * DH)
    return out_seq[position].astype(jnp.bfloat16)
```

```python
import functools
import math

import jax
import jax.numpy as jnp
from jax import lax
from jax.experimental import pallas as pl
from jax.experimental.pallas import tpu as pltpu
from jax.sharding import PartitionSpec as P

DH = 128


def doc_start(position, doc_ends, doc_lengths):
    return jnp.sum(
        jnp.where(doc_ends[None, :] <= position[:, None], doc_lengths[None, :], 0), axis=1
    )


def attend_kernel(
    blocks_ref, q_ref, start_ref, kv_hbm, out_ref, k_buf, v_buf, sems,
    *, half_rows, group_size, kv_feat, pad_rows, window
):
    side = pl.program_id(0)
    head = pl.program_id(1)
    block_id = blocks_ref[side]
    first = pl.multiple_of(block_id * half_rows, half_rows)
    k_copy = pltpu.make_async_copy(
        kv_hbm.at[pl.ds(first, window), pl.ds(pl.multiple_of(head * DH, DH), DH)],
        k_buf,
        sems.at[0],
    )
    v_copy = pltpu.make_async_copy(
        kv_hbm.at[pl.ds(first, window), pl.ds(pl.multiple_of(kv_feat + head * DH, DH), DH)],
        v_buf,
        sems.at[1],
    )
    k_copy.start()
    v_copy.start()
    row_pos = block_id * half_rows + lax.broadcasted_iota(jnp.int32, (half_rows, window), 0)
    key_pos = block_id * half_rows - pad_rows + lax.broadcasted_iota(
        jnp.int32, (half_rows, window), 1
    )
    row_start = start_ref[...]
    allowed = (key_pos <= row_pos) & (key_pos >= row_start)
    bias = jnp.where(allowed, 0.0, -jnp.inf).astype(jnp.float32)
    k_copy.wait()
    v_copy.wait()
    scale = 1.0 / math.sqrt(DH)

    def one_member(g, carry):
        col = pl.multiple_of(g * DH, DH)
        q_g = q_ref[:, pl.ds(col, DH)]
        scores = lax.dot_general(
            q_g, k_buf[...], (((1,), (1,)), ((), ())), preferred_element_type=jnp.float32
        )
        scores = scores * scale + bias
        top = jnp.max(scores, axis=1, keepdims=True)
        weights = jnp.exp(scores - top)
        total = jnp.sum(weights, axis=1, keepdims=True)
        mixed = jnp.dot(
            weights.astype(jnp.bfloat16), v_buf[...], preferred_element_type=jnp.float32
        )
        out_ref[:, pl.ds(col, DH)] = (mixed / total).astype(out_ref.dtype)
        return carry

    lax.fori_loop(0, group_size, one_member, 0)


def on_device(queries, key_rows, value_rows, doc_lengths):
    shards = lax.axis_size("seq")
    kvh = lax.axis_size("kvh")
    my_shard = lax.axis_index("seq")
    rows_in = key_rows.shape[0]
    head_queries = lax.all_to_all(queries, "kvh", split_axis=1, concat_axis=0, tiled=True)
    kv_cols = key_rows.shape[1] // kvh
    kv_local = jnp.concatenate(
        [key_rows.reshape(rows_in, kvh, kv_cols), value_rows.reshape(rows_in, kvh, kv_cols)],
        axis=2,
    )
    kv_slab = lax.all_to_all(kv_local, "kvh", split_axis=1, concat_axis=0, tiled=True)
    dev_rows = kv_slab.shape[0]
    kv_slab = kv_slab.reshape(dev_rows, 2 * kv_cols)
    half_rows = dev_rows // 2
    kv_feat = kv_cols
    kv_heads = kv_feat // DH
    group_size = head_queries.shape[1] // kv_feat
    seq_total = dev_rows * shards
    longest = min(13 * half_rows, seq_total // 4)
    lookback = (longest + half_rows - 2) // half_rows
    pad_rows = lookback * half_rows
    window = pad_rows + half_rows

    gathered = lax.all_gather(kv_slab, "seq", axis=0, tiled=False)
    low = gathered[:, :half_rows].reshape(shards * half_rows, 2 * kv_feat)
    high = gathered[::-1, half_rows:].reshape(shards * half_rows, 2 * kv_feat)
    kv_pos = jnp.concatenate(
        [jnp.zeros((pad_rows, 2 * kv_feat), kv_slab.dtype), low, high], axis=0
    )

    doc_ends = jnp.cumsum(doc_lengths)
    block_ids = jnp.stack([my_shard, 2 * shards - 1 - my_shard]).astype(jnp.int32)
    positions = block_ids[:, None] * half_rows + jnp.arange(half_rows, dtype=jnp.int32)[None, :]
    starts = doc_start(positions.reshape(-1), doc_ends, doc_lengths).astype(jnp.int32)
    starts = starts.reshape(2, half_rows, 1)

    kernel = functools.partial(
        attend_kernel,
        half_rows=half_rows,
        group_size=group_size,
        kv_feat=kv_feat,
        pad_rows=pad_rows,
        window=window,
    )
    q_cols = group_size * DH
    merged = pl.pallas_call(
        kernel,
        out_shape=jax.ShapeDtypeStruct(head_queries.shape, head_queries.dtype),
        grid_spec=pltpu.PrefetchScalarGridSpec(
            num_scalar_prefetch=1,
            grid=(2, kv_heads),
            in_specs=[
                pl.BlockSpec((half_rows, q_cols), lambda s, h, b: (s, h)),
                pl.BlockSpec((None, half_rows, 1), lambda s, h, b: (s, 0, 0)),
                pl.BlockSpec(memory_space=pl.ANY),
            ],
            out_specs=pl.BlockSpec((half_rows, q_cols), lambda s, h, b: (s, h)),
            scratch_shapes=[
                pltpu.VMEM((window, DH), kv_slab.dtype),
                pltpu.VMEM((window, DH), kv_slab.dtype),
                pltpu.SemaphoreType.DMA((2,)),
            ],
        ),
    )(block_ids, head_queries, starts, kv_pos)
    return lax.all_to_all(merged, "kvh", split_axis=0, concat_axis=1, tiled=True)


def solution(mesh):
    return jax.shard_map(
        on_device,
        mesh=mesh,
        in_specs=(P(("seq", "kvh"), None), P(("seq", "kvh"), None), P(("seq", "kvh"), None), P()),
        out_specs=P(("seq", "kvh"), None),
        check_vma=False,
    )
```

```python
import functools
import math

import jax
import jax.numpy as jnp
from jax import lax
from jax.experimental import pallas as pl
from jax.experimental.pallas import tpu as pltpu
from jax.sharding import PartitionSpec as P

DH = 128


def shifted(block, axis, distance):
    devices = range(lax.axis_size(axis))
    route = [(i - distance, i) for i in devices if i - distance in devices]
    return lax.ppermute(block, axis, route)


def doc_start(position, doc_ends, doc_lengths):
    return jnp.sum(
        jnp.where(doc_ends[None, :] <= position[:, None], doc_lengths[None, :], 0), axis=1
    )


def attend_kernel(
    blocks_ref, q_ref, start_ref, k_ref, v_ref, out_ref, kt_buf,
    *, half_rows, group_size, pad_rows, window
):
    side = pl.program_id(0)
    block_id = blocks_ref[side]
    row_pos = block_id * half_rows + lax.broadcasted_iota(jnp.int32, (half_rows, window), 0)
    key_pos = block_id * half_rows - pad_rows + lax.broadcasted_iota(
        jnp.int32, (half_rows, window), 1
    )
    row_start = start_ref[...]
    allowed = (key_pos <= row_pos) & (key_pos >= row_start)
    bias = jnp.where(allowed, 0.0, -jnp.inf).astype(jnp.float32)
    kt_buf[...] = k_ref[...].T
    scale = 1.0 / math.sqrt(DH)

    def one_member(g, carry):
        col = pl.multiple_of(g * DH, DH)
        q_g = q_ref[:, pl.ds(col, DH)]
        scores = jnp.dot(q_g, kt_buf[...], preferred_element_type=jnp.float32)
        scores = scores * scale + bias
        top = jnp.max(scores, axis=1, keepdims=True)
        weights = jnp.exp(scores - top)
        total = jnp.sum(weights, axis=1, keepdims=True)
        mixed = jnp.dot(
            weights.astype(jnp.bfloat16), v_ref[...], preferred_element_type=jnp.float32
        )
        out_ref[:, pl.ds(col, DH)] = (mixed / total).astype(out_ref.dtype)
        return carry

    lax.fori_loop(0, group_size, one_member, 0)


def on_device(queries, key_rows, value_rows, doc_lengths):
    shards = lax.axis_size("seq")
    kvh = lax.axis_size("kvh")
    my_shard = lax.axis_index("seq")
    rows_in = key_rows.shape[0]
    head_queries = lax.all_to_all(queries, "kvh", split_axis=1, concat_axis=0, tiled=True)
    kv_cols = key_rows.shape[1] // kvh
    kv_local = jnp.concatenate(
        [key_rows.reshape(rows_in, kvh, kv_cols), value_rows.reshape(rows_in, kvh, kv_cols)],
        axis=2,
    )
    kv_slab = lax.all_to_all(kv_local, "kvh", split_axis=1, concat_axis=0, tiled=True)
    dev_rows = kv_slab.shape[0]
    kv_slab = kv_slab.reshape(dev_rows, 2 * kv_cols)
    half_rows = dev_rows // 2
    kv_feat = kv_cols
    kv_heads = kv_feat // DH
    group_size = head_queries.shape[1] // kv_feat
    seq_total = dev_rows * shards
    longest = min(13 * half_rows, seq_total // 4)
    lookback = (longest + half_rows - 2) // half_rows
    pad_rows = lookback * half_rows
    window = pad_rows + half_rows

    first_half = kv_slab[:half_rows]
    second_half = kv_slab[half_rows:]
    blank = jnp.zeros_like(first_half)
    low_side = [first_half]
    high_side = [second_half]
    for back in range(1, lookback + 1):
        from_low = shifted(first_half, "seq", back)
        from_high = shifted(second_half, "seq", -back)
        mirror = [(t, 2 * shards - 1 - back - t) for t in range(shards)]
        mirror = [(t, u) for t, u in mirror if 0 <= u < shards and u != t]
        from_mirror = lax.ppermute(first_half, "seq", mirror) if mirror else blank
        wanted = 2 * shards - 1 - my_shard - back
        high_pick = jnp.where(
            wanted >= shards, from_high, jnp.where(wanted == my_shard, first_half, from_mirror)
        )
        low_side.append(from_low)
        high_side.append(high_pick)
    windows = jnp.stack(
        [jnp.concatenate(low_side[::-1], axis=0), jnp.concatenate(high_side[::-1], axis=0)]
    )

    doc_ends = jnp.cumsum(doc_lengths)
    block_ids = jnp.stack([my_shard, 2 * shards - 1 - my_shard]).astype(jnp.int32)
    positions = block_ids[:, None] * half_rows + jnp.arange(half_rows, dtype=jnp.int32)[None, :]
    starts = doc_start(positions.reshape(-1), doc_ends, doc_lengths).astype(jnp.int32)
    starts = starts.reshape(2, half_rows, 1)

    kernel = functools.partial(
        attend_kernel,
        half_rows=half_rows,
        group_size=group_size,
        pad_rows=pad_rows,
        window=window,
    )
    q_cols = group_size * DH
    merged = pl.pallas_call(
        kernel,
        out_shape=jax.ShapeDtypeStruct(head_queries.shape, head_queries.dtype),
        grid_spec=pltpu.PrefetchScalarGridSpec(
            num_scalar_prefetch=1,
            grid=(2, kv_heads),
            in_specs=[
                pl.BlockSpec((half_rows, q_cols), lambda s, h, b: (s, h)),
                pl.BlockSpec((None, half_rows, 1), lambda s, h, b: (s, 0, 0)),
                pl.BlockSpec((None, window, DH), lambda s, h, b: (s, 0, h)),
                pl.BlockSpec((None, window, DH), lambda s, h, b, n=kv_heads: (s, 0, n + h)),
            ],
            out_specs=pl.BlockSpec((half_rows, q_cols), lambda s, h, b: (s, h)),
            scratch_shapes=[
                pltpu.VMEM((DH, window), kv_slab.dtype),
            ],
        ),
    )(block_ids, head_queries, starts, windows, windows)
    return lax.all_to_all(merged, "kvh", split_axis=0, concat_axis=1, tiled=True)


def solution(mesh):
    return jax.shard_map(
        on_device,
        mesh=mesh,
        in_specs=(P(("seq", "kvh"), None), P(("seq", "kvh"), None), P(("seq", "kvh"), None), P()),
        out_specs=P(("seq", "kvh"), None),
        check_vma=False,
    )
```

```python
import functools
import math

import jax
import jax.numpy as jnp
from jax import lax
from jax.experimental import pallas as pl
from jax.experimental.pallas import tpu as pltpu
from jax.sharding import PartitionSpec as P

DH = 128


def shifted(block, axis, distance):
    devices = range(lax.axis_size(axis))
    route = [(i - distance, i) for i in devices if i - distance in devices]
    return lax.ppermute(block, axis, route)


def doc_start(position, doc_ends, doc_lengths):
    return jnp.sum(
        jnp.where(doc_ends[None, :] <= position[:, None], doc_lengths[None, :], 0), axis=1
    )


def attend_kernel(
    blocks_ref, q_ref, start_ref, k_ref, v_ref, out_ref, kt_buf,
    *, half_rows, group_size, pad_rows, window
):
    side = pl.program_id(0)
    block_id = blocks_ref[side]
    needed = blocks_ref[2 + side]
    kt_buf[...] = k_ref[...].T
    scale = 1.0 / math.sqrt(DH)
    row_start = start_ref[...]

    def dense(span):
        skip = window - span
        row_pos = block_id * half_rows + lax.broadcasted_iota(jnp.int32, (half_rows, span), 0)
        key_pos = block_id * half_rows - pad_rows + skip + lax.broadcasted_iota(
            jnp.int32, (half_rows, span), 1
        )
        allowed = (key_pos <= row_pos) & (key_pos >= row_start)
        bias = jnp.where(allowed, 0.0, -jnp.inf).astype(jnp.float32)

        def one_member(g, carry):
            col = pl.multiple_of(g * DH, DH)
            q_g = q_ref[:, pl.ds(col, DH)]
            scores = jnp.dot(q_g, kt_buf[:, skip:], preferred_element_type=jnp.float32)
            scores = scores * scale + bias
            top = jnp.max(scores, axis=1, keepdims=True)
            weights = jnp.exp(scores - top)
            total = jnp.sum(weights, axis=1, keepdims=True)
            mixed = jnp.dot(
                weights.astype(jnp.bfloat16), v_ref[skip:, :], preferred_element_type=jnp.float32
            )
            out_ref[:, pl.ds(col, DH)] = (mixed / total).astype(out_ref.dtype)
            return carry

        lax.fori_loop(0, group_size, one_member, 0)

    for count in range(1, window // half_rows + 1):

        @pl.when(needed == count)
        def _(count=count):
            dense(count * half_rows)


def on_device(queries, key_rows, value_rows, doc_lengths):
    shards = lax.axis_size("seq")
    kvh = lax.axis_size("kvh")
    my_shard = lax.axis_index("seq")
    rows_in = key_rows.shape[0]
    head_queries = lax.all_to_all(queries, "kvh", split_axis=1, concat_axis=0, tiled=True)
    kv_cols = key_rows.shape[1] // kvh
    kv_local = jnp.concatenate(
        [key_rows.reshape(rows_in, kvh, kv_cols), value_rows.reshape(rows_in, kvh, kv_cols)],
        axis=2,
    )
    kv_slab = lax.all_to_all(kv_local, "kvh", split_axis=1, concat_axis=0, tiled=True)
    dev_rows = kv_slab.shape[0]
    kv_slab = kv_slab.reshape(dev_rows, 2 * kv_cols)
    half_rows = dev_rows // 2
    kv_feat = kv_cols
    kv_heads = kv_feat // DH
    group_size = head_queries.shape[1] // kv_feat
    seq_total = dev_rows * shards
    longest = min(13 * half_rows, seq_total // 4)
    lookback = (longest + half_rows - 2) // half_rows
    pad_rows = lookback * half_rows
    window = pad_rows + half_rows

    first_half = kv_slab[:half_rows]
    second_half = kv_slab[half_rows:]
    blank = jnp.zeros_like(first_half)
    low_side = [first_half]
    high_side = [second_half]
    for back in range(1, lookback + 1):
        from_low = shifted(first_half, "seq", back)
        from_high = shifted(second_half, "seq", -back)
        mirror = [(t, 2 * shards - 1 - back - t) for t in range(shards)]
        mirror = [(t, u) for t, u in mirror if 0 <= u < shards and u != t]
        from_mirror = lax.ppermute(first_half, "seq", mirror) if mirror else blank
        wanted = 2 * shards - 1 - my_shard - back
        high_pick = jnp.where(
            wanted >= shards, from_high, jnp.where(wanted == my_shard, first_half, from_mirror)
        )
        low_side.append(from_low)
        high_side.append(high_pick)
    windows = jnp.stack(
        [jnp.concatenate(low_side[::-1], axis=0), jnp.concatenate(high_side[::-1], axis=0)]
    )

    doc_ends = jnp.cumsum(doc_lengths)
    block_ids = jnp.stack([my_shard, 2 * shards - 1 - my_shard]).astype(jnp.int32)
    positions = block_ids[:, None] * half_rows + jnp.arange(half_rows, dtype=jnp.int32)[None, :]
    starts = doc_start(positions.reshape(-1), doc_ends, doc_lengths).astype(jnp.int32)
    needed = 1 + jnp.clip((block_ids * half_rows - starts[::half_rows] + half_rows - 1) // half_rows, 0, lookback)
    block_ids = jnp.concatenate([block_ids, needed.astype(jnp.int32)])
    starts = starts.reshape(2, half_rows, 1)

    kernel = functools.partial(
        attend_kernel,
        half_rows=half_rows,
        group_size=group_size,
        pad_rows=pad_rows,
        window=window,
    )
    q_cols = group_size * DH
    merged = pl.pallas_call(
        kernel,
        out_shape=jax.ShapeDtypeStruct(head_queries.shape, head_queries.dtype),
        grid_spec=pltpu.PrefetchScalarGridSpec(
            num_scalar_prefetch=1,
            grid=(2, kv_heads),
            in_specs=[
                pl.BlockSpec((half_rows, q_cols), lambda s, h, b: (s, h)),
                pl.BlockSpec((None, half_rows, 1), lambda s, h, b: (s, 0, 0)),
                pl.BlockSpec((None, window, DH), lambda s, h, b: (s, 0, h)),
                pl.BlockSpec((None, window, DH), lambda s, h, b, n=kv_heads: (s, 0, n + h)),
            ],
            out_specs=pl.BlockSpec((half_rows, q_cols), lambda s, h, b: (s, h)),
            scratch_shapes=[
                pltpu.VMEM((DH, window), kv_slab.dtype),
            ],
        ),
    )(block_ids, head_queries, starts, windows, windows)
    return lax.all_to_all(merged, "kvh", split_axis=0, concat_axis=1, tiled=True)


def solution(mesh):
    return jax.shard_map(
        on_device,
        mesh=mesh,
        in_specs=(P(("seq", "kvh"), None), P(("seq", "kvh"), None), P(("seq", "kvh"), None), P()),
        out_specs=P(("seq", "kvh"), None),
        check_vma=False,
    )
```

```python
import functools
import math

import jax
import jax.numpy as jnp
from jax import lax
from jax.experimental import pallas as pl
from jax.experimental.pallas import tpu as pltpu
from jax.sharding import PartitionSpec as P

DH = 128


def shifted(block, axis, distance):
    devices = range(lax.axis_size(axis))
    route = [(i - distance, i) for i in devices if i - distance in devices]
    return lax.ppermute(block, axis, route)


def doc_start(position, doc_ends, doc_lengths):
    return jnp.sum(
        jnp.where(doc_ends[None, :] <= position[:, None], doc_lengths[None, :], 0), axis=1
    )


def attend_kernel(
    blocks_ref, q_ref, start_ref, k_ref, v_ref, out_ref, kt_buf,
    *, half_rows, group_size, pad_rows, window
):
    side = pl.program_id(0)
    block_id = blocks_ref[side]
    needed = blocks_ref[2 + side]
    kt_buf[...] = k_ref[...].T
    scale = 1.0 / math.sqrt(DH)
    row_start = start_ref[...]

    def dense(span):
        skip = window - span
        row_pos = block_id * half_rows + lax.broadcasted_iota(jnp.int32, (half_rows, span), 0)
        key_pos = block_id * half_rows - pad_rows + skip + lax.broadcasted_iota(
            jnp.int32, (half_rows, span), 1
        )
        allowed = (key_pos <= row_pos) & (key_pos >= row_start)
        bias = jnp.where(allowed, 0.0, -jnp.inf).astype(jnp.float32)

        def one_member(g, carry):
            col = pl.multiple_of(g * DH, DH)
            q_g = q_ref[:, pl.ds(col, DH)]
            scores = jnp.dot(q_g, kt_buf[:, skip:], preferred_element_type=jnp.float32)
            scores = scores * scale + bias
            top = jnp.max(scores, axis=1, keepdims=True)
            weights = jnp.exp(scores - top)
            total = jnp.sum(weights, axis=1, keepdims=True)
            mixed = jnp.dot(
                weights.astype(jnp.bfloat16), v_ref[skip:, :], preferred_element_type=jnp.float32
            )
            out_ref[:, pl.ds(col, DH)] = (mixed / total).astype(out_ref.dtype)
            return carry

        lax.fori_loop(0, group_size, one_member, 0, unroll=True)

    for count in range(1, window // half_rows + 1):

        @pl.when(needed == count)
        def _(count=count):
            dense(count * half_rows)


def on_device(queries, key_rows, value_rows, doc_lengths):
    shards = lax.axis_size("seq")
    kvh = lax.axis_size("kvh")
    my_shard = lax.axis_index("seq")
    rows_in = key_rows.shape[0]
    head_queries = lax.all_to_all(queries, "kvh", split_axis=1, concat_axis=0, tiled=True)
    kv_cols = key_rows.shape[1] // kvh
    kv_local = jnp.concatenate(
        [key_rows.reshape(rows_in, kvh, kv_cols), value_rows.reshape(rows_in, kvh, kv_cols)],
        axis=2,
    )
    kv_slab = lax.all_to_all(kv_local, "kvh", split_axis=1, concat_axis=0, tiled=True)
    dev_rows = kv_slab.shape[0]
    kv_slab = kv_slab.reshape(dev_rows, 2 * kv_cols)
    half_rows = dev_rows // 2
    kv_feat = kv_cols
    kv_heads = kv_feat // DH
    group_size = head_queries.shape[1] // kv_feat
    seq_total = dev_rows * shards
    longest = min(13 * half_rows, seq_total // 4)
    lookback = (longest + half_rows - 2) // half_rows
    pad_rows = lookback * half_rows
    window = pad_rows + half_rows

    first_half = kv_slab[:half_rows]
    second_half = kv_slab[half_rows:]
    blank = jnp.zeros_like(first_half)
    low_side = [first_half]
    high_side = [second_half]
    for back in range(1, lookback + 1):
        from_low = shifted(first_half, "seq", back)
        from_high = shifted(second_half, "seq", -back)
        mirror = [(t, 2 * shards - 1 - back - t) for t in range(shards)]
        mirror = [(t, u) for t, u in mirror if 0 <= u < shards and u != t]
        from_mirror = lax.ppermute(first_half, "seq", mirror) if mirror else blank
        wanted = 2 * shards - 1 - my_shard - back
        high_pick = jnp.where(
            wanted >= shards, from_high, jnp.where(wanted == my_shard, first_half, from_mirror)
        )
        low_side.append(from_low)
        high_side.append(high_pick)
    windows = jnp.stack(
        [jnp.concatenate(low_side[::-1], axis=0), jnp.concatenate(high_side[::-1], axis=0)]
    )

    doc_ends = jnp.cumsum(doc_lengths)
    block_ids = jnp.stack([my_shard, 2 * shards - 1 - my_shard]).astype(jnp.int32)
    positions = block_ids[:, None] * half_rows + jnp.arange(half_rows, dtype=jnp.int32)[None, :]
    starts = doc_start(positions.reshape(-1), doc_ends, doc_lengths).astype(jnp.int32)
    needed = 1 + jnp.clip((block_ids * half_rows - starts[::half_rows] + half_rows - 1) // half_rows, 0, lookback)
    block_ids = jnp.concatenate([block_ids, needed.astype(jnp.int32)])
    starts = starts.reshape(2, half_rows, 1)

    kernel = functools.partial(
        attend_kernel,
        half_rows=half_rows,
        group_size=group_size,
        pad_rows=pad_rows,
        window=window,
    )
    q_cols = group_size * DH
    merged = pl.pallas_call(
        kernel,
        out_shape=jax.ShapeDtypeStruct(head_queries.shape, head_queries.dtype),
        grid_spec=pltpu.PrefetchScalarGridSpec(
            num_scalar_prefetch=1,
            grid=(2, kv_heads),
            in_specs=[
                pl.BlockSpec((half_rows, q_cols), lambda s, h, b: (s, h)),
                pl.BlockSpec((None, half_rows, 1), lambda s, h, b: (s, 0, 0)),
                pl.BlockSpec((None, window, DH), lambda s, h, b: (s, 0, h)),
                pl.BlockSpec((None, window, DH), lambda s, h, b, n=kv_heads: (s, 0, n + h)),
            ],
            out_specs=pl.BlockSpec((half_rows, q_cols), lambda s, h, b: (s, h)),
            scratch_shapes=[
                pltpu.VMEM((DH, window), kv_slab.dtype),
            ],
        ),
    )(block_ids, head_queries, starts, windows, windows)
    return lax.all_to_all(merged, "kvh", split_axis=0, concat_axis=1, tiled=True)


def solution(mesh):
    return jax.shard_map(
        on_device,
        mesh=mesh,
        in_specs=(P(("seq", "kvh"), None), P(("seq", "kvh"), None), P(("seq", "kvh"), None), P()),
        out_specs=P(("seq", "kvh"), None),
        check_vma=False,
    )
```

```python
import functools
import math

import jax
import jax.numpy as jnp
from jax import lax
from jax.experimental import pallas as pl
from jax.experimental.pallas import tpu as pltpu
from jax.sharding import PartitionSpec as P

DH = 128


def shifted(block, axis, distance):
    devices = range(lax.axis_size(axis))
    route = [(i - distance, i) for i in devices if i - distance in devices]
    return lax.ppermute(block, axis, route)


def doc_start(position, doc_ends, doc_lengths):
    return jnp.sum(
        jnp.where(doc_ends[None, :] <= position[:, None], doc_lengths[None, :], 0), axis=1
    )


def attend_kernel(
    blocks_ref, q_ref, start_ref, k_ref, v_ref, out_ref, kt_buf,
    *, half_rows, group_size, pad_rows, window
):
    block_id = blocks_ref[0]
    needed = blocks_ref[1]
    kt_buf[...] = k_ref[...].T
    scale = 1.0 / math.sqrt(DH)
    row_start = start_ref[...]

    def dense(span):
        skip = window - span
        row_pos = block_id * half_rows + lax.broadcasted_iota(jnp.int32, (half_rows, span), 0)
        key_pos = block_id * half_rows - pad_rows + skip + lax.broadcasted_iota(
            jnp.int32, (half_rows, span), 1
        )
        allowed = (key_pos <= row_pos) & (key_pos >= row_start)
        bias = jnp.where(allowed, 0.0, -jnp.inf).astype(jnp.float32)

        def one_member(g, carry):
            col = pl.multiple_of(g * DH, DH)
            q_g = q_ref[:, pl.ds(col, DH)]
            scores = jnp.dot(q_g, kt_buf[:, skip:], preferred_element_type=jnp.float32)
            scores = scores * scale + bias
            top = jnp.max(scores, axis=1, keepdims=True)
            weights = jnp.exp(scores - top)
            total = jnp.sum(weights, axis=1, keepdims=True)
            mixed = jnp.dot(
                weights.astype(jnp.bfloat16), v_ref[skip:, :], preferred_element_type=jnp.float32
            )
            out_ref[:, pl.ds(col, DH)] = (mixed / total).astype(out_ref.dtype)
            return carry

        lax.fori_loop(0, group_size, one_member, 0, unroll=True)

    for count in range(1, window // half_rows + 1):

        @pl.when(needed == count)
        def _(count=count):
            dense(count * half_rows)


def on_device(queries, key_rows, value_rows, doc_lengths):
    shards = lax.axis_size("seq")
    kvh = lax.axis_size("kvh")
    my_shard = lax.axis_index("seq")
    rows_in = key_rows.shape[0]
    head_queries = lax.all_to_all(queries, "kvh", split_axis=1, concat_axis=0, tiled=True)
    kv_cols = key_rows.shape[1] // kvh
    kv_local = jnp.concatenate(
        [key_rows.reshape(rows_in, kvh, kv_cols), value_rows.reshape(rows_in, kvh, kv_cols)],
        axis=2,
    )
    kv_slab = lax.all_to_all(kv_local, "kvh", split_axis=1, concat_axis=0, tiled=True)
    dev_rows = kv_slab.shape[0]
    kv_slab = kv_slab.reshape(dev_rows, 2 * kv_cols)
    half_rows = dev_rows // 2
    kv_feat = kv_cols
    kv_heads = kv_feat // DH
    group_size = head_queries.shape[1] // kv_feat
    seq_total = dev_rows * shards
    longest = min(13 * half_rows, seq_total // 4)
    lookback = (longest + half_rows - 2) // half_rows
    pad_rows = lookback * half_rows
    window = pad_rows + half_rows

    first_half = kv_slab[:half_rows]
    second_half = kv_slab[half_rows:]
    blank = jnp.zeros_like(first_half)
    low_side = [first_half]
    high_side = [second_half]
    for back in range(1, lookback + 1):
        from_low = shifted(first_half, "seq", back)
        from_high = shifted(second_half, "seq", -back)
        mirror = [(t, 2 * shards - 1 - back - t) for t in range(shards)]
        mirror = [(t, u) for t, u in mirror if 0 <= u < shards and u != t]
        from_mirror = lax.ppermute(first_half, "seq", mirror) if mirror else blank
        wanted = 2 * shards - 1 - my_shard - back
        high_pick = jnp.where(
            wanted >= shards, from_high, jnp.where(wanted == my_shard, first_half, from_mirror)
        )
        low_side.append(from_low)
        high_side.append(high_pick)
    windows = jnp.stack(
        [jnp.concatenate(low_side[::-1], axis=0), jnp.concatenate(high_side[::-1], axis=0)]
    )

    doc_ends = jnp.cumsum(doc_lengths)
    block_ids = jnp.stack([my_shard, 2 * shards - 1 - my_shard]).astype(jnp.int32)
    positions = block_ids[:, None] * half_rows + jnp.arange(half_rows, dtype=jnp.int32)[None, :]
    starts = doc_start(positions.reshape(-1), doc_ends, doc_lengths).astype(jnp.int32)
    needed = 1 + jnp.clip((block_ids * half_rows - starts[::half_rows] + half_rows - 1) // half_rows, 0, lookback)
    block_ids = jnp.concatenate([block_ids, needed.astype(jnp.int32)])
    starts = starts.reshape(2, half_rows, 1)

    kernel = functools.partial(
        attend_kernel,
        half_rows=half_rows,
        group_size=group_size,
        pad_rows=pad_rows,
        window=window,
    )
    q_cols = group_size * DH
    my_head = lax.axis_index("kvh")
    half_dev = kvh // 2
    piece_cols = head_queries.shape[1]
    backs = []
    for side_no in range(2):
        side_out = pl.pallas_call(
            kernel,
            out_shape=jax.ShapeDtypeStruct((half_rows, piece_cols), head_queries.dtype),
            grid_spec=pltpu.PrefetchScalarGridSpec(
                num_scalar_prefetch=1,
                grid=(kv_heads,),
                in_specs=[
                    pl.BlockSpec((half_rows, q_cols), lambda h, b, s=side_no: (s, h)),
                    pl.BlockSpec((half_rows, 1), lambda h, b: (0, 0)),
                    pl.BlockSpec((window, DH), lambda h, b: (0, h)),
                    pl.BlockSpec((window, DH), lambda h, b, n=kv_heads: (0, n + h)),
                ],
                out_specs=pl.BlockSpec((half_rows, q_cols), lambda h, b: (0, h)),
                scratch_shapes=[
                    pltpu.VMEM((DH, window), kv_slab.dtype),
                ],
            ),
        )(
            jnp.stack([block_ids[side_no], block_ids[2 + side_no]]),
            head_queries,
            starts[side_no],
            windows[side_no],
            windows[side_no],
        )
        pieces = []
        for shift in range(kvh):
            dest = (my_head + shift) % kvh
            piece = lax.dynamic_slice_in_dim(side_out, (dest % half_dev) * rows_in, rows_in, 0)
            if shift:
                route = [
                    (j, (j + shift) % kvh) for j in range(kvh) if (j + shift) % kvh // half_dev == side_no
                ]
                piece = lax.ppermute(piece, "kvh", route)
            pieces.append(piece)
        backs.append(jnp.stack(pieces))
    mine = jnp.where(my_head < half_dev, backs[0], backs[1])
    order = (my_head - jnp.arange(kvh)) % kvh
    return jnp.take(mine, order, axis=0).transpose(1, 0, 2).reshape(rows_in, kvh * piece_cols)


def solution(mesh):
    return jax.shard_map(
        on_device,
        mesh=mesh,
        in_specs=(P(("seq", "kvh"), None), P(("seq", "kvh"), None), P(("seq", "kvh"), None), P()),
        out_specs=P(("seq", "kvh"), None),
        check_vma=False,
    )
```

```python
import functools
import math

import jax
import jax.numpy as jnp
from jax import lax
from jax.experimental import pallas as pl
from jax.experimental.pallas import tpu as pltpu
from jax.sharding import PartitionSpec as P

DH = 128


def shifted(block, axis, distance):
    devices = range(lax.axis_size(axis))
    route = [(i - distance, i) for i in devices if i - distance in devices]
    return lax.ppermute(block, axis, route)


def doc_start(position, doc_ends, doc_lengths):
    return jnp.sum(
        jnp.where(doc_ends[None, :] <= position[:, None], doc_lengths[None, :], 0), axis=1
    )


def attend_kernel(
    table_ref, q_ref, start_ref, k_ref, v_ref, out_ref, kt_buf,
    *, sub_rows, n_chunks, half_rows, group_size, pad_rows, window
):
    chunk = pl.program_id(0)
    first_pos = table_ref[chunk]
    needed = table_ref[n_chunks + chunk]
    block_start = table_ref[3 * n_chunks + chunk]
    kt_buf[...] = k_ref[...].T
    scale = 1.0 / math.sqrt(DH)
    row_start = start_ref[...]

    def dense(span):
        skip = window - span
        row_pos = first_pos + lax.broadcasted_iota(jnp.int32, (sub_rows, span), 0)
        key_pos = block_start - pad_rows + skip + lax.broadcasted_iota(
            jnp.int32, (sub_rows, span), 1
        )
        allowed = (key_pos <= row_pos) & (key_pos >= row_start)
        bias = jnp.where(allowed, 0.0, -jnp.inf).astype(jnp.float32)

        def one_member(g, carry):
            col = pl.multiple_of(g * DH, DH)
            q_g = q_ref[:, pl.ds(col, DH)]
            scores = jnp.dot(q_g, kt_buf[:, skip:], preferred_element_type=jnp.float32)
            scores = scores * scale + bias
            top = jnp.max(scores, axis=1, keepdims=True)
            weights = jnp.exp(scores - top)
            total = jnp.sum(weights, axis=1, keepdims=True)
            mixed = jnp.dot(
                weights.astype(jnp.bfloat16), v_ref[skip:, :], preferred_element_type=jnp.float32
            )
            out_ref[:, pl.ds(col, DH)] = (mixed / total).astype(out_ref.dtype)
            return carry

        lax.fori_loop(0, group_size, one_member, 0, unroll=True)

    for count in range(1, window // half_rows + 1):

        @pl.when(needed == count)
        def _(count=count):
            dense(count * half_rows)


def on_device(queries, key_rows, value_rows, doc_lengths):
    shards = lax.axis_size("seq")
    kvh = lax.axis_size("kvh")
    my_shard = lax.axis_index("seq")
    rows_in = key_rows.shape[0]
    head_queries = lax.all_to_all(queries, "kvh", split_axis=1, concat_axis=0, tiled=True)
    kv_cols = key_rows.shape[1] // kvh
    kv_local = jnp.concatenate(
        [key_rows.reshape(rows_in, kvh, kv_cols), value_rows.reshape(rows_in, kvh, kv_cols)],
        axis=2,
    )
    kv_slab = lax.all_to_all(kv_local, "kvh", split_axis=1, concat_axis=0, tiled=True)
    dev_rows = kv_slab.shape[0]
    kv_slab = kv_slab.reshape(dev_rows, 2 * kv_cols)
    half_rows = dev_rows // 2
    kv_feat = kv_cols
    kv_heads = kv_feat // DH
    group_size = head_queries.shape[1] // kv_feat
    seq_total = dev_rows * shards
    longest = min(13 * half_rows, seq_total // 4)
    lookback = (longest + half_rows - 2) // half_rows
    pad_rows = lookback * half_rows
    window = pad_rows + half_rows

    first_half = kv_slab[:half_rows]
    second_half = kv_slab[half_rows:]
    blank = jnp.zeros_like(first_half)
    low_side = [first_half]
    high_side = [second_half]
    for back in range(1, lookback + 1):
        from_low = shifted(first_half, "seq", back)
        from_high = shifted(second_half, "seq", -back)
        mirror = [(t, 2 * shards - 1 - back - t) for t in range(shards)]
        mirror = [(t, u) for t, u in mirror if 0 <= u < shards and u != t]
        from_mirror = lax.ppermute(first_half, "seq", mirror) if mirror else blank
        wanted = 2 * shards - 1 - my_shard - back
        high_pick = jnp.where(
            wanted >= shards, from_high, jnp.where(wanted == my_shard, first_half, from_mirror)
        )
        low_side.append(from_low)
        high_side.append(high_pick)
    windows = jnp.stack(
        [jnp.concatenate(low_side[::-1], axis=0), jnp.concatenate(high_side[::-1], axis=0)]
    )

    doc_ends = jnp.cumsum(doc_lengths)
    sub_rows = rows_in // 2
    chunk_no = jnp.arange(kvh, dtype=jnp.int32)
    side_of = chunk_no // (kvh // 2)
    block_of = jnp.where(side_of == 0, my_shard, 2 * shards - 1 - my_shard).astype(jnp.int32)
    block_start = block_of * half_rows
    chunk_pos = block_start + (chunk_no % (kvh // 2)) * rows_in

    kernel = functools.partial(
        attend_kernel,
        sub_rows=sub_rows,
        n_chunks=kvh,
        half_rows=half_rows,
        group_size=group_size,
        pad_rows=pad_rows,
        window=window,
    )
    q_cols = group_size * DH
    results = []
    for part in range(2):
        first_pos = chunk_pos + part * sub_rows
        positions = first_pos[:, None] + jnp.arange(sub_rows, dtype=jnp.int32)[None, :]
        starts = doc_start(positions.reshape(-1), doc_ends, doc_lengths).astype(jnp.int32)
        starts = starts.reshape(kvh, sub_rows)
        needed = 1 + jnp.clip((block_start - starts[:, 0] + half_rows - 1) // half_rows, 0, lookback)
        table = jnp.concatenate([first_pos, needed, side_of, block_start]).astype(jnp.int32)
        out_part = pl.pallas_call(
            kernel,
            out_shape=jax.ShapeDtypeStruct((kvh * sub_rows, head_queries.shape[1]), head_queries.dtype),
            grid_spec=pltpu.PrefetchScalarGridSpec(
                num_scalar_prefetch=1,
                grid=(kvh, kv_heads),
                in_specs=[
                    pl.BlockSpec((sub_rows, q_cols), lambda c, h, t, p=part: (2 * c + p, h)),
                    pl.BlockSpec((None, sub_rows, 1), lambda c, h, t: (c, 0, 0)),
                    pl.BlockSpec(
                        (None, window, DH), lambda c, h, t, n=kvh: (t[2 * n + c], 0, h)
                    ),
                    pl.BlockSpec(
                        (None, window, DH),
                        lambda c, h, t, n=kvh, m=kv_heads: (t[2 * n + c], 0, m + h),
                    ),
                ],
                out_specs=pl.BlockSpec((sub_rows, q_cols), lambda c, h, t: (c, h)),
                scratch_shapes=[
                    pltpu.VMEM((DH, window), kv_slab.dtype),
                ],
            ),
        )(table, head_queries, starts.reshape(kvh, sub_rows, 1), windows, windows)
        results.append(lax.all_to_all(out_part, "kvh", split_axis=0, concat_axis=1, tiled=True))
    return jnp.concatenate(results, axis=0)


def solution(mesh):
    return jax.shard_map(
        on_device,
        mesh=mesh,
        in_specs=(P(("seq", "kvh"), None), P(("seq", "kvh"), None), P(("seq", "kvh"), None), P()),
        out_specs=P(("seq", "kvh"), None),
        check_vma=False,
    )
```

```python
import functools
import math

import jax
import jax.numpy as jnp
from jax import lax
from jax.experimental import pallas as pl
from jax.experimental.pallas import tpu as pltpu
from jax.sharding import PartitionSpec as P

DH = 128


def shifted(block, axis, distance):
    devices = range(lax.axis_size(axis))
    route = [(i - distance, i) for i in devices if i - distance in devices]
    return lax.ppermute(block, axis, route)


def doc_start(position, doc_ends, doc_lengths):
    return jnp.sum(
        jnp.where(doc_ends[None, :] <= position[:, None], doc_lengths[None, :], 0), axis=1
    )


def attend_kernel(
    blocks_ref, q_ref, start_ref, k_ref, v_ref, out_ref, kt_buf,
    *, half_rows, group_size, pad_rows, window
):
    side = pl.program_id(0)
    block_id = blocks_ref[side]
    needed = blocks_ref[2 + side]
    kt_buf[...] = k_ref[...].T
    scale = 1.0 / math.sqrt(DH)
    row_start = start_ref[...]

    def dense(span):
        skip = window - span
        row_pos = block_id * half_rows + lax.broadcasted_iota(jnp.int32, (half_rows, span), 0)
        key_pos = block_id * half_rows - pad_rows + skip + lax.broadcasted_iota(
            jnp.int32, (half_rows, span), 1
        )
        allowed = (key_pos <= row_pos) & (key_pos >= row_start)
        bias = jnp.where(allowed, 0.0, -jnp.inf).astype(jnp.float32)

        def one_member(g, carry):
            col = pl.multiple_of(g * DH, DH)
            q_g = q_ref[:, pl.ds(col, DH)]
            scores = jnp.dot(q_g, kt_buf[:, skip:], preferred_element_type=jnp.float32)
            scores = scores * scale + bias
            top = jnp.max(scores, axis=1, keepdims=True)
            weights = jnp.exp(scores - top)
            total = jnp.sum(weights, axis=1, keepdims=True)
            mixed = jnp.dot(
                weights.astype(jnp.bfloat16), v_ref[skip:, :], preferred_element_type=jnp.float32
            )
            out_ref[:, pl.ds(col, DH)] = (mixed / total).astype(out_ref.dtype)
            return carry

        lax.fori_loop(0, group_size, one_member, 0, unroll=True)

    for count in range(1, window // half_rows + 1):

        @pl.when(needed == count)
        def _(count=count):
            dense(count * half_rows)


def on_device(queries, key_rows, value_rows, doc_lengths):
    shards = lax.axis_size("seq")
    kvh = lax.axis_size("kvh")
    my_shard = lax.axis_index("seq")
    rows_in = key_rows.shape[0]
    head_queries = lax.all_to_all(queries, "kvh", split_axis=1, concat_axis=0, tiled=True)
    kv_cols = key_rows.shape[1] // kvh
    kv_local = jnp.concatenate(
        [key_rows.reshape(rows_in, kvh, kv_cols), value_rows.reshape(rows_in, kvh, kv_cols)],
        axis=2,
    )
    kv_slab = lax.all_to_all(kv_local, "kvh", split_axis=1, concat_axis=0, tiled=True)
    dev_rows = kv_slab.shape[0]
    kv_slab = kv_slab.reshape(dev_rows, 2 * kv_cols)
    half_rows = dev_rows // 2
    kv_feat = kv_cols
    kv_heads = kv_feat // DH
    group_size = head_queries.shape[1] // kv_feat
    seq_total = dev_rows * shards
    longest = min(13 * half_rows, seq_total // 4)
    lookback = (longest + half_rows - 2) // half_rows
    pad_rows = lookback * half_rows
    window = pad_rows + half_rows

    reach = min(lookback, shards - 1)
    received = [shifted(kv_slab, "seq", back) for back in range(reach, 0, -1)]
    received += [kv_slab] + [shifted(kv_slab, "seq", -ahead) for ahead in range(1, reach + 1)]
    stacked = jnp.stack(received)
    low_side = [kv_slab[:half_rows]]
    high_side = [kv_slab[half_rows:]]
    for back in range(1, lookback + 1):
        if back <= reach:
            low_side.append(received[reach - back][:half_rows])
        else:
            low_side.append(jnp.zeros_like(low_side[0]))
        wanted = 2 * shards - 1 - my_shard - back
        ahead = min(back, reach)
        upper = received[reach + ahead][half_rows:]
        slot = jnp.clip(reach + wanted - my_shard, 0, 2 * reach)
        mirrored = lax.dynamic_index_in_dim(stacked, slot, 0, keepdims=False)[:half_rows]
        high_side.append(jnp.where(wanted >= shards, upper, mirrored))
    windows = jnp.stack(
        [jnp.concatenate(low_side[::-1], axis=0), jnp.concatenate(high_side[::-1], axis=0)]
    )

    doc_ends = jnp.cumsum(doc_lengths)
    block_ids = jnp.stack([my_shard, 2 * shards - 1 - my_shard]).astype(jnp.int32)
    positions = block_ids[:, None] * half_rows + jnp.arange(half_rows, dtype=jnp.int32)[None, :]
    starts = doc_start(positions.reshape(-1), doc_ends, doc_lengths).astype(jnp.int32)
    needed = 1 + jnp.clip((block_ids * half_rows - starts[::half_rows] + half_rows - 1) // half_rows, 0, lookback)
    block_ids = jnp.concatenate([block_ids, needed.astype(jnp.int32)])
    starts = starts.reshape(2, half_rows, 1)

    kernel = functools.partial(
        attend_kernel,
        half_rows=half_rows,
        group_size=group_size,
        pad_rows=pad_rows,
        window=window,
    )
    q_cols = group_size * DH
    merged = pl.pallas_call(
        kernel,
        out_shape=jax.ShapeDtypeStruct(head_queries.shape, head_queries.dtype),
        grid_spec=pltpu.PrefetchScalarGridSpec(
            num_scalar_prefetch=1,
            grid=(2, kv_heads),
            in_specs=[
                pl.BlockSpec((half_rows, q_cols), lambda s, h, b: (s, h)),
                pl.BlockSpec((None, half_rows, 1), lambda s, h, b: (s, 0, 0)),
                pl.BlockSpec((None, window, DH), lambda s, h, b: (s, 0, h)),
                pl.BlockSpec((None, window, DH), lambda s, h, b, n=kv_heads: (s, 0, n + h)),
            ],
            out_specs=pl.BlockSpec((half_rows, q_cols), lambda s, h, b: (s, h)),
            scratch_shapes=[
                pltpu.VMEM((DH, window), kv_slab.dtype),
            ],
        ),
    )(block_ids, head_queries, starts, windows, windows)
    return lax.all_to_all(merged, "kvh", split_axis=0, concat_axis=1, tiled=True)


def solution(mesh):
    return jax.shard_map(
        on_device,
        mesh=mesh,
        in_specs=(P(("seq", "kvh"), None), P(("seq", "kvh"), None), P(("seq", "kvh"), None), P()),
        out_specs=P(("seq", "kvh"), None),
        check_vma=False,
    )
```

```python
import functools
import math

import jax
import jax.numpy as jnp
from jax import lax
from jax.experimental import pallas as pl
from jax.experimental.pallas import tpu as pltpu
from jax.sharding import PartitionSpec as P

DH = 128


def shifted(block, axis, distance):
    devices = range(lax.axis_size(axis))
    route = [(i - distance, i) for i in devices if i - distance in devices]
    return lax.ppermute(block, axis, route)


def doc_start(position, doc_ends, doc_lengths):
    return jnp.sum(
        jnp.where(doc_ends[None, :] <= position[:, None], doc_lengths[None, :], 0), axis=1
    )


def attend_kernel(
    blocks_ref, q_ref, start_ref, k_ref, v_ref, out_ref, kt_buf,
    *, half_rows, group_size, pad_rows, window
):
    side = pl.program_id(0)
    block_id = blocks_ref[side]
    needed = blocks_ref[2 + side]
    kt_buf[...] = k_ref[...].T
    scale = 1.0 / math.sqrt(DH)
    row_start = start_ref[...]

    def dense(span):
        skip = window - span
        row_pos = block_id * half_rows + lax.broadcasted_iota(jnp.int32, (half_rows, span), 0)
        key_pos = block_id * half_rows - pad_rows + skip + lax.broadcasted_iota(
            jnp.int32, (half_rows, span), 1
        )
        allowed = (key_pos <= row_pos) & (key_pos >= row_start)
        bias = jnp.where(allowed, 0.0, -jnp.inf).astype(jnp.float32)

        def one_member(g, carry):
            col = pl.multiple_of(g * DH, DH)
            q_g = q_ref[:, pl.ds(col, DH)]
            scores = jnp.dot(q_g, kt_buf[:, skip:], preferred_element_type=jnp.float32)
            scores = scores * scale + bias
            top = jnp.max(scores, axis=1, keepdims=True)
            weights = jnp.exp(scores - top)
            total = jnp.sum(weights, axis=1, keepdims=True)
            mixed = jnp.dot(
                weights.astype(jnp.bfloat16), v_ref[skip:, :], preferred_element_type=jnp.float32
            )
            out_ref[:, pl.ds(col, DH)] = (mixed / total).astype(out_ref.dtype)
            return carry

        lax.fori_loop(0, group_size, one_member, 0, unroll=True)

    for count in range(1, window // half_rows + 1):

        @pl.when(needed == count)
        def _(count=count):
            dense(count * half_rows)


def on_device(queries, key_rows, value_rows, doc_lengths):
    shards = lax.axis_size("seq")
    kvh = lax.axis_size("kvh")
    my_shard = lax.axis_index("seq")
    rows_in = key_rows.shape[0]
    head_queries = lax.all_to_all(queries, "kvh", split_axis=1, concat_axis=0, tiled=True)
    kv_cols = key_rows.shape[1] // kvh
    kv_local = jnp.concatenate(
        [key_rows.reshape(rows_in, kvh, kv_cols), value_rows.reshape(rows_in, kvh, kv_cols)],
        axis=2,
    )
    kv_slab = lax.all_to_all(kv_local, "kvh", split_axis=1, concat_axis=0, tiled=True)
    dev_rows = kv_slab.shape[0]
    kv_slab = kv_slab.reshape(dev_rows, 2 * kv_cols)
    half_rows = dev_rows // 2
    kv_feat = kv_cols
    kv_heads = kv_feat // DH
    group_size = head_queries.shape[1] // kv_feat
    seq_total = dev_rows * shards
    longest = min(13 * half_rows, seq_total // 4)
    lookback = (longest + half_rows - 2) // half_rows
    pad_rows = lookback * half_rows
    window = pad_rows + half_rows

    first_half = kv_slab[:half_rows]
    second_half = kv_slab[half_rows:]
    blank = jnp.zeros_like(first_half)
    low_side = [first_half]
    high_side = [second_half]
    for back in range(1, lookback + 1):
        from_low = shifted(first_half, "seq", back)
        from_high = shifted(second_half, "seq", -back)
        mirror = [(t, 2 * shards - 1 - back - t) for t in range(shards)]
        mirror = [(t, u) for t, u in mirror if 0 <= u < shards and u != t]
        from_mirror = lax.ppermute(first_half, "seq", mirror) if mirror else blank
        wanted = 2 * shards - 1 - my_shard - back
        high_pick = jnp.where(
            wanted >= shards, from_high, jnp.where(wanted == my_shard, first_half, from_mirror)
        )
        low_side.append(from_low)
        high_side.append(high_pick)
    windows = jnp.stack(
        [jnp.concatenate(low_side[::-1], axis=0), jnp.concatenate(high_side[::-1], axis=0)]
    )

    doc_ends = jnp.cumsum(doc_lengths)
    block_ids = jnp.stack([my_shard, 2 * shards - 1 - my_shard]).astype(jnp.int32)
    positions = block_ids[:, None] * half_rows + jnp.arange(half_rows, dtype=jnp.int32)[None, :]
    starts = doc_start(positions.reshape(-1), doc_ends, doc_lengths).astype(jnp.int32)
    needed = 1 + jnp.clip((block_ids * half_rows - starts[::half_rows] + half_rows - 1) // half_rows, 0, lookback)
    block_ids = jnp.concatenate([block_ids, needed.astype(jnp.int32)])
    starts = starts.reshape(2, half_rows, 1)

    kernel = functools.partial(
        attend_kernel,
        half_rows=half_rows,
        group_size=group_size,
        pad_rows=pad_rows,
        window=window,
    )
    q_cols = group_size * DH
    per_head = []
    for head_no in range(kv_heads):
        head_out = pl.pallas_call(
            kernel,
            out_shape=jax.ShapeDtypeStruct((dev_rows, q_cols), head_queries.dtype),
            grid_spec=pltpu.PrefetchScalarGridSpec(
                num_scalar_prefetch=1,
                grid=(2,),
                in_specs=[
                    pl.BlockSpec((half_rows, q_cols), lambda s, b, h=head_no: (s, h)),
                    pl.BlockSpec((None, half_rows, 1), lambda s, b: (s, 0, 0)),
                    pl.BlockSpec((None, window, DH), lambda s, b, h=head_no: (s, 0, h)),
                    pl.BlockSpec(
                        (None, window, DH), lambda s, b, h=head_no, n=kv_heads: (s, 0, n + h)
                    ),
                ],
                out_specs=pl.BlockSpec((half_rows, q_cols), lambda s, b: (s, 0)),
                scratch_shapes=[
                    pltpu.VMEM((DH, window), kv_slab.dtype),
                ],
            ),
        )(block_ids, head_queries, starts, windows, windows)
        back = lax.all_to_all(head_out, "kvh", split_axis=0, concat_axis=1, tiled=True)
        per_head.append(back.reshape(rows_in, kvh, q_cols))
    return jnp.stack(per_head, axis=2).reshape(rows_in, kvh * kv_heads * q_cols)


def solution(mesh):
    return jax.shard_map(
        on_device,
        mesh=mesh,
        in_specs=(P(("seq", "kvh"), None), P(("seq", "kvh"), None), P(("seq", "kvh"), None), P()),
        out_specs=P(("seq", "kvh"), None),
        check_vma=False,
    )
```

```python
import functools
import math

import jax
import jax.numpy as jnp
from jax import lax
from jax.experimental import pallas as pl
from jax.experimental.pallas import tpu as pltpu
from jax.sharding import PartitionSpec as P

DH = 128


def shifted(block, axis, distance):
    devices = range(lax.axis_size(axis))
    route = [(i - distance, i) for i in devices if i - distance in devices]
    return lax.ppermute(block, axis, route)


def doc_start(position, doc_ends, doc_lengths):
    return jnp.sum(
        jnp.where(doc_ends[None, :] <= position[:, None], doc_lengths[None, :], 0), axis=1
    )


def attend_kernel(
    blocks_ref, q_ref, start_ref, k_ref, v_ref, out_ref, kt_buf,
    *, half_rows, group_size, pad_rows, window
):
    side = pl.program_id(0)
    block_id = blocks_ref[side]
    needed = blocks_ref[2 + side]
    kt_buf[...] = k_ref[...].T
    scale = 1.0 / math.sqrt(DH)
    row_start = start_ref[...]

    def dense(span):
        skip = window - span
        row_pos = block_id * half_rows + lax.broadcasted_iota(jnp.int32, (half_rows, span), 0)
        key_pos = block_id * half_rows - pad_rows + skip + lax.broadcasted_iota(
            jnp.int32, (half_rows, span), 1
        )
        allowed = (key_pos <= row_pos) & (key_pos >= row_start)
        bias = jnp.where(allowed, 0.0, -jnp.inf).astype(jnp.float32)

        def one_member(g, carry):
            col = pl.multiple_of(g * DH, DH)
            q_g = q_ref[:, pl.ds(col, DH)]
            scores = jnp.dot(q_g, kt_buf[:, skip:], preferred_element_type=jnp.float32)
            scores = scores * scale + bias
            top = jnp.max(scores, axis=1, keepdims=True)
            weights = jnp.exp(scores - top)
            total = jnp.sum(weights, axis=1, keepdims=True)
            mixed = jnp.dot(
                weights.astype(jnp.bfloat16), v_ref[skip:, :], preferred_element_type=jnp.float32
            )
            out_ref[:, pl.ds(col, DH)] = (mixed / total).astype(out_ref.dtype)
            return carry

        lax.fori_loop(0, group_size, one_member, 0, unroll=True)

    for count in range(1, window // half_rows + 1):

        @pl.when(needed == count)
        def _(count=count):
            dense(count * half_rows)


def interleave_kernel(*refs, q_cols):
    out_ref = refs[-1]
    for head_no, part_ref in enumerate(refs[:-1]):
        out_ref[:, head_no * q_cols : (head_no + 1) * q_cols] = part_ref[...]


def on_device(queries, key_rows, value_rows, doc_lengths):
    shards = lax.axis_size("seq")
    kvh = lax.axis_size("kvh")
    my_shard = lax.axis_index("seq")
    rows_in = key_rows.shape[0]
    head_queries = lax.all_to_all(queries, "kvh", split_axis=1, concat_axis=0, tiled=True)
    kv_cols = key_rows.shape[1] // kvh
    kv_local = jnp.concatenate(
        [key_rows.reshape(rows_in, kvh, kv_cols), value_rows.reshape(rows_in, kvh, kv_cols)],
        axis=2,
    )
    kv_slab = lax.all_to_all(kv_local, "kvh", split_axis=1, concat_axis=0, tiled=True)
    dev_rows = kv_slab.shape[0]
    kv_slab = kv_slab.reshape(dev_rows, 2 * kv_cols)
    half_rows = dev_rows // 2
    kv_feat = kv_cols
    kv_heads = kv_feat // DH
    group_size = head_queries.shape[1] // kv_feat
    seq_total = dev_rows * shards
    longest = min(13 * half_rows, seq_total // 4)
    lookback = (longest + half_rows - 2) // half_rows
    pad_rows = lookback * half_rows
    window = pad_rows + half_rows

    first_half = kv_slab[:half_rows]
    second_half = kv_slab[half_rows:]
    blank = jnp.zeros_like(first_half)
    low_side = [first_half]
    high_side = [second_half]
    for back in range(1, lookback + 1):
        from_low = shifted(first_half, "seq", back)
        from_high = shifted(second_half, "seq", -back)
        mirror = [(t, 2 * shards - 1 - back - t) for t in range(shards)]
        mirror = [(t, u) for t, u in mirror if 0 <= u < shards and u != t]
        from_mirror = lax.ppermute(first_half, "seq", mirror) if mirror else blank
        wanted = 2 * shards - 1 - my_shard - back
        high_pick = jnp.where(
            wanted >= shards, from_high, jnp.where(wanted == my_shard, first_half, from_mirror)
        )
        low_side.append(from_low)
        high_side.append(high_pick)
    windows = jnp.stack(
        [jnp.concatenate(low_side[::-1], axis=0), jnp.concatenate(high_side[::-1], axis=0)]
    )

    doc_ends = jnp.cumsum(doc_lengths)
    block_ids = jnp.stack([my_shard, 2 * shards - 1 - my_shard]).astype(jnp.int32)
    positions = block_ids[:, None] * half_rows + jnp.arange(half_rows, dtype=jnp.int32)[None, :]
    starts = doc_start(positions.reshape(-1), doc_ends, doc_lengths).astype(jnp.int32)
    needed = 1 + jnp.clip((block_ids * half_rows - starts[::half_rows] + half_rows - 1) // half_rows, 0, lookback)
    block_ids = jnp.concatenate([block_ids, needed.astype(jnp.int32)])
    starts = starts.reshape(2, half_rows, 1)

    kernel = functools.partial(
        attend_kernel,
        half_rows=half_rows,
        group_size=group_size,
        pad_rows=pad_rows,
        window=window,
    )
    q_cols = group_size * DH
    per_head = []
    for head_no in range(kv_heads):
        head_out = pl.pallas_call(
            kernel,
            out_shape=jax.ShapeDtypeStruct((dev_rows, q_cols), head_queries.dtype),
            grid_spec=pltpu.PrefetchScalarGridSpec(
                num_scalar_prefetch=1,
                grid=(2,),
                in_specs=[
                    pl.BlockSpec((half_rows, q_cols), lambda s, b, h=head_no: (s, h)),
                    pl.BlockSpec((None, half_rows, 1), lambda s, b: (s, 0, 0)),
                    pl.BlockSpec((None, window, DH), lambda s, b, h=head_no: (s, 0, h)),
                    pl.BlockSpec(
                        (None, window, DH), lambda s, b, h=head_no, n=kv_heads: (s, 0, n + h)
                    ),
                ],
                out_specs=pl.BlockSpec((half_rows, q_cols), lambda s, b: (s, 0)),
                scratch_shapes=[
                    pltpu.VMEM((DH, window), kv_slab.dtype),
                ],
            ),
        )(block_ids, head_queries, starts, windows, windows)
        per_head.append(
            lax.all_to_all(
                head_out.reshape(kvh, rows_in, q_cols), "kvh", split_axis=0, concat_axis=0, tiled=True
            )
        )
    if kv_heads == 1:
        return per_head[0].transpose(1, 0, 2).reshape(rows_in, kvh * q_cols)
    return pl.pallas_call(
        functools.partial(interleave_kernel, q_cols=q_cols),
        out_shape=jax.ShapeDtypeStruct((rows_in, kvh * kv_heads * q_cols), head_queries.dtype),
        grid=(kvh,),
        in_specs=[pl.BlockSpec((None, rows_in, q_cols), lambda j: (j, 0, 0))] * kv_heads,
        out_specs=pl.BlockSpec((rows_in, kv_heads * q_cols), lambda j: (0, j)),
    )(*per_head)


def solution(mesh):
    return jax.shard_map(
        on_device,
        mesh=mesh,
        in_specs=(P(("seq", "kvh"), None), P(("seq", "kvh"), None), P(("seq", "kvh"), None), P()),
        out_specs=P(("seq", "kvh"), None),
        check_vma=False,
    )
```

```python
import functools
import math

import jax
import jax.numpy as jnp
from jax import lax
from jax.experimental import pallas as pl
from jax.experimental.pallas import tpu as pltpu
from jax.sharding import PartitionSpec as P

DH = 128


def shifted(block, axis, distance):
    devices = range(lax.axis_size(axis))
    route = [(i - distance, i) for i in devices if i - distance in devices]
    return lax.ppermute(block, axis, route)


def doc_start(position, doc_ends, doc_lengths):
    return jnp.sum(
        jnp.where(doc_ends[None, :] <= position[:, None], doc_lengths[None, :], 0), axis=1
    )


def attend_kernel(
    blocks_ref, q_ref, start_ref, k_ref, v_ref, out_ref, kt_buf, v_buf,
    *, half_rows, group_size, pad_rows, window
):
    side = pl.program_id(0)
    block_id = blocks_ref[side]
    needed = blocks_ref[2 + side]
    kt_buf[...] = k_ref[...].T
    v_buf[:, :DH] = v_ref[...]
    lane = lax.broadcasted_iota(jnp.int32, (window, DH), 1)
    v_buf[:, DH:] = jnp.where(lane == 0, 1.0, 0.0).astype(v_buf.dtype)
    scale = 1.0 / math.sqrt(DH)
    row_start = start_ref[...]

    def dense(span):
        skip = window - span
        row_pos = block_id * half_rows + lax.broadcasted_iota(jnp.int32, (half_rows, span), 0)
        key_pos = block_id * half_rows - pad_rows + skip + lax.broadcasted_iota(
            jnp.int32, (half_rows, span), 1
        )
        allowed = (key_pos <= row_pos) & (key_pos >= row_start)
        bias = jnp.where(allowed, 0.0, -jnp.inf).astype(jnp.float32)

        def one_member(g, carry):
            col = pl.multiple_of(g * DH, DH)
            q_g = q_ref[:, pl.ds(col, DH)]
            scores = jnp.dot(q_g, kt_buf[:, skip:], preferred_element_type=jnp.float32)
            scores = scores * scale + bias
            top = jnp.max(scores, axis=1, keepdims=True)
            weights = jnp.exp(scores - top)
            mixed = jnp.dot(
                weights.astype(jnp.bfloat16), v_buf[skip:, :], preferred_element_type=jnp.float32
            )
            total = mixed[:, DH : DH + 1]
            out_ref[:, pl.ds(col, DH)] = (mixed[:, :DH] / total).astype(out_ref.dtype)
            return carry

        lax.fori_loop(0, group_size, one_member, 0, unroll=True)

    for count in range(1, window // half_rows + 1):

        @pl.when(needed == count)
        def _(count=count):
            dense(count * half_rows)


def on_device(queries, key_rows, value_rows, doc_lengths):
    shards = lax.axis_size("seq")
    kvh = lax.axis_size("kvh")
    my_shard = lax.axis_index("seq")
    rows_in = key_rows.shape[0]
    head_queries = lax.all_to_all(queries, "kvh", split_axis=1, concat_axis=0, tiled=True)
    kv_cols = key_rows.shape[1] // kvh
    kv_local = jnp.concatenate(
        [key_rows.reshape(rows_in, kvh, kv_cols), value_rows.reshape(rows_in, kvh, kv_cols)],
        axis=2,
    )
    kv_slab = lax.all_to_all(kv_local, "kvh", split_axis=1, concat_axis=0, tiled=True)
    dev_rows = kv_slab.shape[0]
    kv_slab = kv_slab.reshape(dev_rows, 2 * kv_cols)
    half_rows = dev_rows // 2
    kv_feat = kv_cols
    kv_heads = kv_feat // DH
    group_size = head_queries.shape[1] // kv_feat
    seq_total = dev_rows * shards
    longest = min(13 * half_rows, seq_total // 4)
    lookback = (longest + half_rows - 2) // half_rows
    pad_rows = lookback * half_rows
    window = pad_rows + half_rows

    first_half = kv_slab[:half_rows]
    second_half = kv_slab[half_rows:]
    blank = jnp.zeros_like(first_half)
    low_side = [first_half]
    high_side = [second_half]
    for back in range(1, lookback + 1):
        from_low = shifted(first_half, "seq", back)
        from_high = shifted(second_half, "seq", -back)
        mirror = [(t, 2 * shards - 1 - back - t) for t in range(shards)]
        mirror = [(t, u) for t, u in mirror if 0 <= u < shards and u != t]
        from_mirror = lax.ppermute(first_half, "seq", mirror) if mirror else blank
        wanted = 2 * shards - 1 - my_shard - back
        high_pick = jnp.where(
            wanted >= shards, from_high, jnp.where(wanted == my_shard, first_half, from_mirror)
        )
        low_side.append(from_low)
        high_side.append(high_pick)
    windows = jnp.stack(
        [jnp.concatenate(low_side[::-1], axis=0), jnp.concatenate(high_side[::-1], axis=0)]
    )

    doc_ends = jnp.cumsum(doc_lengths)
    block_ids = jnp.stack([my_shard, 2 * shards - 1 - my_shard]).astype(jnp.int32)
    positions = block_ids[:, None] * half_rows + jnp.arange(half_rows, dtype=jnp.int32)[None, :]
    starts = doc_start(positions.reshape(-1), doc_ends, doc_lengths).astype(jnp.int32)
    needed = 1 + jnp.clip((block_ids * half_rows - starts[::half_rows] + half_rows - 1) // half_rows, 0, lookback)
    block_ids = jnp.concatenate([block_ids, needed.astype(jnp.int32)])
    starts = starts.reshape(2, half_rows, 1)

    kernel = functools.partial(
        attend_kernel,
        half_rows=half_rows,
        group_size=group_size,
        pad_rows=pad_rows,
        window=window,
    )
    q_cols = group_size * DH
    merged = pl.pallas_call(
        kernel,
        out_shape=jax.ShapeDtypeStruct(head_queries.shape, head_queries.dtype),
        grid_spec=pltpu.PrefetchScalarGridSpec(
            num_scalar_prefetch=1,
            grid=(2, kv_heads),
            in_specs=[
                pl.BlockSpec((half_rows, q_cols), lambda s, h, b: (s, h)),
                pl.BlockSpec((None, half_rows, 1), lambda s, h, b: (s, 0, 0)),
                pl.BlockSpec((None, window, DH), lambda s, h, b: (s, 0, h)),
                pl.BlockSpec((None, window, DH), lambda s, h, b, n=kv_heads: (s, 0, n + h)),
            ],
            out_specs=pl.BlockSpec((half_rows, q_cols), lambda s, h, b: (s, h)),
            scratch_shapes=[
                pltpu.VMEM((DH, window), kv_slab.dtype),
                pltpu.VMEM((window, 2 * DH), kv_slab.dtype),
            ],
        ),
    )(block_ids, head_queries, starts, windows, windows)
    return lax.all_to_all(merged, "kvh", split_axis=0, concat_axis=1, tiled=True)


def solution(mesh):
    return jax.shard_map(
        on_device,
        mesh=mesh,
        in_specs=(P(("seq", "kvh"), None), P(("seq", "kvh"), None), P(("seq", "kvh"), None), P()),
        out_specs=P(("seq", "kvh"), None),
        check_vma=False,
    )
```

```python
import functools
import math

import jax
import jax.numpy as jnp
from jax import lax
from jax.experimental import pallas as pl
from jax.experimental.pallas import tpu as pltpu
from jax.sharding import PartitionSpec as P

DH = 128


def shifted(block, axis, distance):
    devices = range(lax.axis_size(axis))
    route = [(i - distance, i) for i in devices if i - distance in devices]
    return lax.ppermute(block, axis, route)


def doc_start(position, doc_ends, doc_lengths):
    return jnp.sum(
        jnp.where(doc_ends[None, :] <= position[:, None], doc_lengths[None, :], 0), axis=1
    )


def attend_kernel(
    blocks_ref, q_ref, start_ref, k_ref, v_ref, out_ref, kt_buf, v_buf,
    *, half_rows, group_size, pad_rows, window
):
    side = pl.program_id(0)
    block_id = blocks_ref[side]
    kt_buf[...] = k_ref[...].T
    v_buf[:, :DH] = v_ref[...]
    lane = lax.broadcasted_iota(jnp.int32, (window, DH), 1)
    v_buf[:, DH:] = jnp.where(lane == 0, 1.0, 0.0).astype(v_buf.dtype)
    scale = 1.0 / math.sqrt(DH)
    sub_rows = half_rows // 2

    def dense(part, count):
        lo = pad_rows - (count - 1) * half_rows
        hi = pad_rows + (part + 1) * sub_rows
        span = hi - lo
        rows = slice(part * sub_rows, (part + 1) * sub_rows)
        row_pos = block_id * half_rows + part * sub_rows + lax.broadcasted_iota(
            jnp.int32, (sub_rows, span), 0
        )
        key_pos = block_id * half_rows - pad_rows + lo + lax.broadcasted_iota(
            jnp.int32, (sub_rows, span), 1
        )
        allowed = (key_pos <= row_pos) & (key_pos >= start_ref[rows, :])
        bias = jnp.where(allowed, 0.0, -jnp.inf).astype(jnp.float32)

        def one_member(g, carry):
            col = pl.multiple_of(g * DH, DH)
            q_g = q_ref[rows, pl.ds(col, DH)]
            scores = jnp.dot(q_g, kt_buf[:, lo:hi], preferred_element_type=jnp.float32)
            scores = scores * scale + bias
            top = jnp.max(scores, axis=1, keepdims=True)
            weights = jnp.exp(scores - top)
            mixed = jnp.dot(
                weights.astype(jnp.bfloat16), v_buf[lo:hi, :], preferred_element_type=jnp.float32
            )
            total = mixed[:, DH : DH + 1]
            out_ref[rows, pl.ds(col, DH)] = (mixed[:, :DH] / total).astype(out_ref.dtype)
            return carry

        lax.fori_loop(0, group_size, one_member, 0, unroll=True)

    for part in range(2):
        needed = blocks_ref[2 + 2 * side + part]
        for count in range(1, window // half_rows + 1):

            @pl.when(needed == count)
            def _(part=part, count=count):
                dense(part, count)


def on_device(queries, key_rows, value_rows, doc_lengths):
    shards = lax.axis_size("seq")
    kvh = lax.axis_size("kvh")
    my_shard = lax.axis_index("seq")
    rows_in = key_rows.shape[0]
    head_queries = lax.all_to_all(queries, "kvh", split_axis=1, concat_axis=0, tiled=True)
    kv_cols = key_rows.shape[1] // kvh
    kv_local = jnp.concatenate(
        [key_rows.reshape(rows_in, kvh, kv_cols), value_rows.reshape(rows_in, kvh, kv_cols)],
        axis=2,
    )
    kv_slab = lax.all_to_all(kv_local, "kvh", split_axis=1, concat_axis=0, tiled=True)
    dev_rows = kv_slab.shape[0]
    kv_slab = kv_slab.reshape(dev_rows, 2 * kv_cols)
    half_rows = dev_rows // 2
    kv_feat = kv_cols
    kv_heads = kv_feat // DH
    group_size = head_queries.shape[1] // kv_feat
    seq_total = dev_rows * shards
    longest = min(13 * half_rows, seq_total // 4)
    lookback = (longest + half_rows - 2) // half_rows
    pad_rows = lookback * half_rows
    window = pad_rows + half_rows

    first_half = kv_slab[:half_rows]
    second_half = kv_slab[half_rows:]
    blank = jnp.zeros_like(first_half)
    low_side = [first_half]
    high_side = [second_half]
    for back in range(1, lookback + 1):
        from_low = shifted(first_half, "seq", back)
        from_high = shifted(second_half, "seq", -back)
        mirror = [(t, 2 * shards - 1 - back - t) for t in range(shards)]
        mirror = [(t, u) for t, u in mirror if 0 <= u < shards and u != t]
        from_mirror = lax.ppermute(first_half, "seq", mirror) if mirror else blank
        wanted = 2 * shards - 1 - my_shard - back
        high_pick = jnp.where(
            wanted >= shards, from_high, jnp.where(wanted == my_shard, first_half, from_mirror)
        )
        low_side.append(from_low)
        high_side.append(high_pick)
    windows = jnp.stack(
        [jnp.concatenate(low_side[::-1], axis=0), jnp.concatenate(high_side[::-1], axis=0)]
    )

    doc_ends = jnp.cumsum(doc_lengths)
    block_ids = jnp.stack([my_shard, 2 * shards - 1 - my_shard]).astype(jnp.int32)
    positions = block_ids[:, None] * half_rows + jnp.arange(half_rows, dtype=jnp.int32)[None, :]
    starts = doc_start(positions.reshape(-1), doc_ends, doc_lengths).astype(jnp.int32)
    sub_rows = half_rows // 2
    firsts = starts.reshape(2, 2, sub_rows)[:, :, 0]
    needed = 1 + jnp.clip(
        (block_ids[:, None] * half_rows - firsts + half_rows - 1) // half_rows, 0, lookback
    )
    block_ids = jnp.concatenate([block_ids, needed.reshape(-1).astype(jnp.int32)])
    starts = starts.reshape(2, half_rows, 1)

    kernel = functools.partial(
        attend_kernel,
        half_rows=half_rows,
        group_size=group_size,
        pad_rows=pad_rows,
        window=window,
    )
    q_cols = group_size * DH
    merged = pl.pallas_call(
        kernel,
        out_shape=jax.ShapeDtypeStruct(head_queries.shape, head_queries.dtype),
        grid_spec=pltpu.PrefetchScalarGridSpec(
            num_scalar_prefetch=1,
            grid=(2, kv_heads),
            in_specs=[
                pl.BlockSpec((half_rows, q_cols), lambda s, h, b: (s, h)),
                pl.BlockSpec((None, half_rows, 1), lambda s, h, b: (s, 0, 0)),
                pl.BlockSpec((None, window, DH), lambda s, h, b: (s, 0, h)),
                pl.BlockSpec((None, window, DH), lambda s, h, b, n=kv_heads: (s, 0, n + h)),
            ],
            out_specs=pl.BlockSpec((half_rows, q_cols), lambda s, h, b: (s, h)),
            scratch_shapes=[
                pltpu.VMEM((DH, window), kv_slab.dtype),
                pltpu.VMEM((window, 2 * DH), kv_slab.dtype),
            ],
        ),
    )(block_ids, head_queries, starts, windows, windows)
    return lax.all_to_all(merged, "kvh", split_axis=0, concat_axis=1, tiled=True)


def solution(mesh):
    return jax.shard_map(
        on_device,
        mesh=mesh,
        in_specs=(P(("seq", "kvh"), None), P(("seq", "kvh"), None), P(("seq", "kvh"), None), P()),
        out_specs=P(("seq", "kvh"), None),
        check_vma=False,
    )
```

```python
import functools
import math

import jax
import jax.numpy as jnp
from jax import lax
from jax.experimental import pallas as pl
from jax.experimental.pallas import tpu as pltpu
from jax.sharding import PartitionSpec as P

DH = 128


def shifted(block, axis, distance):
    devices = range(lax.axis_size(axis))
    route = [(i - distance, i) for i in devices if i - distance in devices]
    return lax.ppermute(block, axis, route)


def doc_start(position, doc_ends, doc_lengths):
    return jnp.sum(
        jnp.where(doc_ends[None, :] <= position[:, None], doc_lengths[None, :], 0), axis=1
    )


def attend_kernel(
    blocks_ref, q_ref, start_ref, k_ref, v_ref, out_ref, kt_buf, v_buf,
    *, half_rows, group_size, pad_rows, window
):
    side = pl.program_id(0)
    block_id = blocks_ref[side]
    needed = blocks_ref[2 + side]
    kt_buf[...] = k_ref[...].T
    v_buf[:, :DH] = v_ref[...]
    lane = lax.broadcasted_iota(jnp.int32, (window, DH), 1)
    v_buf[:, DH:] = jnp.where(lane == 0, 1.0, 0.0).astype(v_buf.dtype)
    scale = 1.0 / math.sqrt(DH)
    row_start = start_ref[...]

    def dense(span):
        skip = window - span
        row_pos = block_id * half_rows + lax.broadcasted_iota(jnp.int32, (half_rows, span), 0)
        key_pos = block_id * half_rows - pad_rows + skip + lax.broadcasted_iota(
            jnp.int32, (half_rows, span), 1
        )
        allowed = (key_pos <= row_pos) & (key_pos >= row_start)
        bias = jnp.where(allowed, 0.0, -jnp.inf).astype(jnp.float32)

        def one_pair(pair, carry):
            cols = [pl.multiple_of((2 * pair + i) * DH, DH) for i in range(2)]
            q_two = jnp.concatenate([q_ref[:, pl.ds(c, DH)] for c in cols], axis=0)
            scores = jnp.dot(q_two, kt_buf[:, skip:], preferred_element_type=jnp.float32)
            scores = scores.reshape(2, half_rows, span) * scale + bias[None]
            top = jnp.max(scores, axis=2, keepdims=True)
            weights = jnp.exp(scores - top).reshape(2 * half_rows, span)
            mixed = jnp.dot(
                weights.astype(jnp.bfloat16), v_buf[skip:, :], preferred_element_type=jnp.float32
            )
            normed = mixed[:, :DH] / mixed[:, DH : DH + 1]
            for i in range(2):
                out_ref[:, pl.ds(cols[i], DH)] = normed[i * half_rows : (i + 1) * half_rows].astype(
                    out_ref.dtype
                )
            return carry

        lax.fori_loop(0, group_size // 2, one_pair, 0, unroll=True)

    for count in range(1, window // half_rows + 1):

        @pl.when(needed == count)
        def _(count=count):
            dense(count * half_rows)


def on_device(queries, key_rows, value_rows, doc_lengths):
    shards = lax.axis_size("seq")
    kvh = lax.axis_size("kvh")
    my_shard = lax.axis_index("seq")
    rows_in = key_rows.shape[0]
    head_queries = lax.all_to_all(queries, "kvh", split_axis=1, concat_axis=0, tiled=True)
    kv_cols = key_rows.shape[1] // kvh
    kv_local = jnp.concatenate(
        [key_rows.reshape(rows_in, kvh, kv_cols), value_rows.reshape(rows_in, kvh, kv_cols)],
        axis=2,
    )
    kv_slab = lax.all_to_all(kv_local, "kvh", split_axis=1, concat_axis=0, tiled=True)
    dev_rows = kv_slab.shape[0]
    kv_slab = kv_slab.reshape(dev_rows, 2 * kv_cols)
    half_rows = dev_rows // 2
    kv_feat = kv_cols
    kv_heads = kv_feat // DH
    group_size = head_queries.shape[1] // kv_feat
    seq_total = dev_rows * shards
    longest = min(13 * half_rows, seq_total // 4)
    lookback = (longest + half_rows - 2) // half_rows
    pad_rows = lookback * half_rows
    window = pad_rows + half_rows

    first_half = kv_slab[:half_rows]
    second_half = kv_slab[half_rows:]
    blank = jnp.zeros_like(first_half)
    low_side = [first_half]
    high_side = [second_half]
    for back in range(1, lookback + 1):
        from_low = shifted(first_half, "seq", back)
        from_high = shifted(second_half, "seq", -back)
        mirror = [(t, 2 * shards - 1 - back - t) for t in range(shards)]
        mirror = [(t, u) for t, u in mirror if 0 <= u < shards and u != t]
        from_mirror = lax.ppermute(first_half, "seq", mirror) if mirror else blank
        wanted = 2 * shards - 1 - my_shard - back
        high_pick = jnp.where(
            wanted >= shards, from_high, jnp.where(wanted == my_shard, first_half, from_mirror)
        )
        low_side.append(from_low)
        high_side.append(high_pick)
    windows = jnp.stack(
        [jnp.concatenate(low_side[::-1], axis=0), jnp.concatenate(high_side[::-1], axis=0)]
    )

    doc_ends = jnp.cumsum(doc_lengths)
    block_ids = jnp.stack([my_shard, 2 * shards - 1 - my_shard]).astype(jnp.int32)
    positions = block_ids[:, None] * half_rows + jnp.arange(half_rows, dtype=jnp.int32)[None, :]
    starts = doc_start(positions.reshape(-1), doc_ends, doc_lengths).astype(jnp.int32)
    needed = 1 + jnp.clip((block_ids * half_rows - starts[::half_rows] + half_rows - 1) // half_rows, 0, lookback)
    block_ids = jnp.concatenate([block_ids, needed.astype(jnp.int32)])
    starts = starts.reshape(2, half_rows, 1)

    kernel = functools.partial(
        attend_kernel,
        half_rows=half_rows,
        group_size=group_size,
        pad_rows=pad_rows,
        window=window,
    )
    q_cols = group_size * DH
    merged = pl.pallas_call(
        kernel,
        out_shape=jax.ShapeDtypeStruct(head_queries.shape, head_queries.dtype),
        grid_spec=pltpu.PrefetchScalarGridSpec(
            num_scalar_prefetch=1,
            grid=(2, kv_heads),
            in_specs=[
                pl.BlockSpec((half_rows, q_cols), lambda s, h, b: (s, h)),
                pl.BlockSpec((None, half_rows, 1), lambda s, h, b: (s, 0, 0)),
                pl.BlockSpec((None, window, DH), lambda s, h, b: (s, 0, h)),
                pl.BlockSpec((None, window, DH), lambda s, h, b, n=kv_heads: (s, 0, n + h)),
            ],
            out_specs=pl.BlockSpec((half_rows, q_cols), lambda s, h, b: (s, h)),
            scratch_shapes=[
                pltpu.VMEM((DH, window), kv_slab.dtype),
                pltpu.VMEM((window, 2 * DH), kv_slab.dtype),
            ],
        ),
    )(block_ids, head_queries, starts, windows, windows)
    return lax.all_to_all(merged, "kvh", split_axis=0, concat_axis=1, tiled=True)


def solution(mesh):
    return jax.shard_map(
        on_device,
        mesh=mesh,
        in_specs=(P(("seq", "kvh"), None), P(("seq", "kvh"), None), P(("seq", "kvh"), None), P()),
        out_specs=P(("seq", "kvh"), None),
        check_vma=False,
    )
```

```python
import functools
import math

import jax
import jax.numpy as jnp
from jax import lax
from jax.experimental import pallas as pl
from jax.experimental.pallas import tpu as pltpu
from jax.sharding import PartitionSpec as P

DH = 128
BUNCH = 4


def shifted(block, axis, distance):
    devices = range(lax.axis_size(axis))
    route = [(i - distance, i) for i in devices if i - distance in devices]
    return lax.ppermute(block, axis, route)


def doc_start(position, doc_ends, doc_lengths):
    return jnp.sum(
        jnp.where(doc_ends[None, :] <= position[:, None], doc_lengths[None, :], 0), axis=1
    )


def attend_kernel(
    blocks_ref, q_ref, start_ref, k_ref, v_ref, out_ref, kt_buf, v_buf,
    *, half_rows, group_size, pad_rows, window
):
    side = pl.program_id(0)
    block_id = blocks_ref[side]
    needed = blocks_ref[2 + side]
    kt_buf[...] = k_ref[...].T
    v_buf[:, :DH] = v_ref[...]
    lane = lax.broadcasted_iota(jnp.int32, (window, DH), 1)
    v_buf[:, DH:] = jnp.where(lane == 0, 1.0, 0.0).astype(v_buf.dtype)
    scale = 1.0 / math.sqrt(DH)
    row_start = start_ref[...]

    def dense(span):
        skip = window - span
        row_pos = block_id * half_rows + lax.broadcasted_iota(jnp.int32, (half_rows, span), 0)
        key_pos = block_id * half_rows - pad_rows + skip + lax.broadcasted_iota(
            jnp.int32, (half_rows, span), 1
        )
        allowed = (key_pos <= row_pos) & (key_pos >= row_start)
        bias = jnp.where(allowed, 0.0, -jnp.inf).astype(jnp.float32)

        def one_pair(pair, carry):
            cols = [pl.multiple_of((BUNCH * pair + i) * DH, DH) for i in range(BUNCH)]
            q_two = jnp.concatenate([q_ref[:, pl.ds(c, DH)] for c in cols], axis=0)
            scores = jnp.dot(q_two, kt_buf[:, skip:], preferred_element_type=jnp.float32)
            scores = scores.reshape(BUNCH, half_rows, span) * scale + bias[None]
            top = jnp.max(scores, axis=2, keepdims=True)
            weights = jnp.exp(scores - top).reshape(BUNCH * half_rows, span)
            mixed = jnp.dot(
                weights.astype(jnp.bfloat16), v_buf[skip:, :], preferred_element_type=jnp.float32
            )
            normed = mixed[:, :DH] / mixed[:, DH : DH + 1]
            for i in range(BUNCH):
                out_ref[:, pl.ds(cols[i], DH)] = normed[i * half_rows : (i + 1) * half_rows].astype(
                    out_ref.dtype
                )
            return carry

        lax.fori_loop(0, group_size // BUNCH, one_pair, 0, unroll=True)

    for count in range(1, window // half_rows + 1):

        @pl.when(needed == count)
        def _(count=count):
            dense(count * half_rows)


def on_device(queries, key_rows, value_rows, doc_lengths):
    shards = lax.axis_size("seq")
    kvh = lax.axis_size("kvh")
    my_shard = lax.axis_index("seq")
    rows_in = key_rows.shape[0]
    head_queries = lax.all_to_all(queries, "kvh", split_axis=1, concat_axis=0, tiled=True)
    kv_cols = key_rows.shape[1] // kvh
    kv_local = jnp.concatenate(
        [key_rows.reshape(rows_in, kvh, kv_cols), value_rows.reshape(rows_in, kvh, kv_cols)],
        axis=2,
    )
    kv_slab = lax.all_to_all(kv_local, "kvh", split_axis=1, concat_axis=0, tiled=True)
    dev_rows = kv_slab.shape[0]
    kv_slab = kv_slab.reshape(dev_rows, 2 * kv_cols)
    half_rows = dev_rows // 2
    kv_feat = kv_cols
    kv_heads = kv_feat // DH
    group_size = head_queries.shape[1] // kv_feat
    seq_total = dev_rows * shards
    longest = min(13 * half_rows, seq_total // 4)
    lookback = (longest + half_rows - 2) // half_rows
    pad_rows = lookback * half_rows
    window = pad_rows + half_rows

    first_half = kv_slab[:half_rows]
    second_half = kv_slab[half_rows:]
    blank = jnp.zeros_like(first_half)
    low_side = [first_half]
    high_side = [second_half]
    for back in range(1, lookback + 1):
        from_low = shifted(first_half, "seq", back)
        from_high = shifted(second_half, "seq", -back)
        mirror = [(t, 2 * shards - 1 - back - t) for t in range(shards)]
        mirror = [(t, u) for t, u in mirror if 0 <= u < shards and u != t]
        from_mirror = lax.ppermute(first_half, "seq", mirror) if mirror else blank
        wanted = 2 * shards - 1 - my_shard - back
        high_pick = jnp.where(
            wanted >= shards, from_high, jnp.where(wanted == my_shard, first_half, from_mirror)
        )
        low_side.append(from_low)
        high_side.append(high_pick)
    windows = jnp.stack(
        [jnp.concatenate(low_side[::-1], axis=0), jnp.concatenate(high_side[::-1], axis=0)]
    )

    doc_ends = jnp.cumsum(doc_lengths)
    block_ids = jnp.stack([my_shard, 2 * shards - 1 - my_shard]).astype(jnp.int32)
    positions = block_ids[:, None] * half_rows + jnp.arange(half_rows, dtype=jnp.int32)[None, :]
    starts = doc_start(positions.reshape(-1), doc_ends, doc_lengths).astype(jnp.int32)
    needed = 1 + jnp.clip((block_ids * half_rows - starts[::half_rows] + half_rows - 1) // half_rows, 0, lookback)
    block_ids = jnp.concatenate([block_ids, needed.astype(jnp.int32)])
    starts = starts.reshape(2, half_rows, 1)

    kernel = functools.partial(
        attend_kernel,
        half_rows=half_rows,
        group_size=group_size,
        pad_rows=pad_rows,
        window=window,
    )
    q_cols = group_size * DH
    merged = pl.pallas_call(
        kernel,
        out_shape=jax.ShapeDtypeStruct(head_queries.shape, head_queries.dtype),
        grid_spec=pltpu.PrefetchScalarGridSpec(
            num_scalar_prefetch=1,
            grid=(2, kv_heads),
            in_specs=[
                pl.BlockSpec((half_rows, q_cols), lambda s, h, b: (s, h)),
                pl.BlockSpec((None, half_rows, 1), lambda s, h, b: (s, 0, 0)),
                pl.BlockSpec((None, window, DH), lambda s, h, b: (s, 0, h)),
                pl.BlockSpec((None, window, DH), lambda s, h, b, n=kv_heads: (s, 0, n + h)),
            ],
            out_specs=pl.BlockSpec((half_rows, q_cols), lambda s, h, b: (s, h)),
            scratch_shapes=[
                pltpu.VMEM((DH, window), kv_slab.dtype),
                pltpu.VMEM((window, 2 * DH), kv_slab.dtype),
            ],
        ),
    )(block_ids, head_queries, starts, windows, windows)
    return lax.all_to_all(merged, "kvh", split_axis=0, concat_axis=1, tiled=True)


def solution(mesh):
    return jax.shard_map(
        on_device,
        mesh=mesh,
        in_specs=(P(("seq", "kvh"), None), P(("seq", "kvh"), None), P(("seq", "kvh"), None), P()),
        out_specs=P(("seq", "kvh"), None),
        check_vma=False,
    )
```

```python
import functools
import math

import jax
import jax.numpy as jnp
from jax import lax
from jax.experimental import pallas as pl
from jax.experimental.pallas import tpu as pltpu
from jax.sharding import PartitionSpec as P

DH = 128
BUNCH = 4


def shifted(block, axis, distance):
    devices = range(lax.axis_size(axis))
    route = [(i - distance, i) for i in devices if i - distance in devices]
    return lax.ppermute(block, axis, route)


def doc_start(position, doc_ends, doc_lengths):
    return jnp.sum(
        jnp.where(doc_ends[None, :] <= position[:, None], doc_lengths[None, :], 0), axis=1
    )


def attend_kernel(
    blocks_ref, q_ref, start_ref, kt_buf, v_buf, out_ref,
    *, half_rows, group_size, pad_rows, window
):
    side = pl.program_id(0)
    block_id = blocks_ref[side]
    needed = blocks_ref[2 + side]
    scale = 1.0 / math.sqrt(DH)
    row_start = start_ref[...]

    def dense(span):
        skip = window - span
        row_pos = block_id * half_rows + lax.broadcasted_iota(jnp.int32, (half_rows, span), 0)
        key_pos = block_id * half_rows - pad_rows + skip + lax.broadcasted_iota(
            jnp.int32, (half_rows, span), 1
        )
        allowed = (key_pos <= row_pos) & (key_pos >= row_start)
        bias = jnp.where(allowed, 0.0, -jnp.inf).astype(jnp.float32)

        def one_pair(pair, carry):
            cols = [pl.multiple_of((BUNCH * pair + i) * DH, DH) for i in range(BUNCH)]
            q_two = jnp.concatenate([q_ref[:, pl.ds(c, DH)] for c in cols], axis=0)
            scores = jnp.dot(q_two, kt_buf[:, skip:], preferred_element_type=jnp.float32)
            scores = scores.reshape(BUNCH, half_rows, span) * scale + bias[None]
            top = jnp.max(scores, axis=2, keepdims=True)
            weights = jnp.exp(scores - top).reshape(BUNCH * half_rows, span)
            mixed = jnp.dot(
                weights.astype(jnp.bfloat16), v_buf[skip:, :], preferred_element_type=jnp.float32
            )
            normed = mixed[:, :DH] / mixed[:, DH : DH + 1]
            for i in range(BUNCH):
                out_ref[:, pl.ds(cols[i], DH)] = normed[i * half_rows : (i + 1) * half_rows].astype(
                    out_ref.dtype
                )
            return carry

        lax.fori_loop(0, group_size // BUNCH, one_pair, 0, unroll=True)

    for count in range(1, window // half_rows + 1):

        @pl.when(needed == count)
        def _(count=count):
            dense(count * half_rows)


def on_device(queries, key_rows, value_rows, doc_lengths):
    shards = lax.axis_size("seq")
    kvh = lax.axis_size("kvh")
    my_shard = lax.axis_index("seq")
    rows_in = key_rows.shape[0]
    head_queries = lax.all_to_all(queries, "kvh", split_axis=1, concat_axis=0, tiled=True)
    kv_cols = key_rows.shape[1] // kvh
    kv_local = jnp.concatenate(
        [key_rows.reshape(rows_in, kvh, kv_cols), value_rows.reshape(rows_in, kvh, kv_cols)],
        axis=2,
    )
    kv_slab = lax.all_to_all(kv_local, "kvh", split_axis=1, concat_axis=0, tiled=True)
    dev_rows = kv_slab.shape[0]
    kv_slab = kv_slab.reshape(dev_rows, 2 * kv_cols)
    half_rows = dev_rows // 2
    kv_feat = kv_cols
    kv_heads = kv_feat // DH
    group_size = head_queries.shape[1] // kv_feat
    seq_total = dev_rows * shards
    longest = min(13 * half_rows, seq_total // 4)
    lookback = (longest + half_rows - 2) // half_rows
    pad_rows = lookback * half_rows
    window = pad_rows + half_rows

    first_half = kv_slab[:half_rows]
    second_half = kv_slab[half_rows:]
    blank = jnp.zeros_like(first_half)
    low_side = [first_half]
    high_side = [second_half]
    for back in range(1, lookback + 1):
        from_low = shifted(first_half, "seq", back)
        from_high = shifted(second_half, "seq", -back)
        mirror = [(t, 2 * shards - 1 - back - t) for t in range(shards)]
        mirror = [(t, u) for t, u in mirror if 0 <= u < shards and u != t]
        from_mirror = lax.ppermute(first_half, "seq", mirror) if mirror else blank
        wanted = 2 * shards - 1 - my_shard - back
        high_pick = jnp.where(
            wanted >= shards, from_high, jnp.where(wanted == my_shard, first_half, from_mirror)
        )
        low_side.append(from_low)
        high_side.append(high_pick)
    windows = jnp.stack(
        [jnp.concatenate(low_side[::-1], axis=0), jnp.concatenate(high_side[::-1], axis=0)]
    )

    keys_t = windows[:, :, :kv_feat].transpose(0, 2, 1)
    values = windows[:, :, kv_feat:].reshape(2, window, kv_heads, DH)
    ones = jnp.zeros_like(values).at[..., 0].set(1)
    values_ext = jnp.concatenate([values, ones], axis=3).reshape(2, window, kv_heads * 2 * DH)
    doc_ends = jnp.cumsum(doc_lengths)
    block_ids = jnp.stack([my_shard, 2 * shards - 1 - my_shard]).astype(jnp.int32)
    positions = block_ids[:, None] * half_rows + jnp.arange(half_rows, dtype=jnp.int32)[None, :]
    starts = doc_start(positions.reshape(-1), doc_ends, doc_lengths).astype(jnp.int32)
    needed = 1 + jnp.clip((block_ids * half_rows - starts[::half_rows] + half_rows - 1) // half_rows, 0, lookback)
    block_ids = jnp.concatenate([block_ids, needed.astype(jnp.int32)])
    starts = starts.reshape(2, half_rows, 1)

    kernel = functools.partial(
        attend_kernel,
        half_rows=half_rows,
        group_size=group_size,
        pad_rows=pad_rows,
        window=window,
    )
    q_cols = group_size * DH
    merged = pl.pallas_call(
        kernel,
        out_shape=jax.ShapeDtypeStruct(head_queries.shape, head_queries.dtype),
        grid_spec=pltpu.PrefetchScalarGridSpec(
            num_scalar_prefetch=1,
            grid=(2, kv_heads),
            in_specs=[
                pl.BlockSpec((half_rows, q_cols), lambda s, h, b: (s, h)),
                pl.BlockSpec((None, half_rows, 1), lambda s, h, b: (s, 0, 0)),
                pl.BlockSpec((None, DH, window), lambda s, h, b: (s, h, 0)),
                pl.BlockSpec((None, window, 2 * DH), lambda s, h, b: (s, 0, h)),
            ],
            out_specs=pl.BlockSpec((half_rows, q_cols), lambda s, h, b: (s, h)),
        ),
    )(block_ids, head_queries, starts, keys_t, values_ext)
    return lax.all_to_all(merged, "kvh", split_axis=0, concat_axis=1, tiled=True)


def solution(mesh):
    return jax.shard_map(
        on_device,
        mesh=mesh,
        in_specs=(P(("seq", "kvh"), None), P(("seq", "kvh"), None), P(("seq", "kvh"), None), P()),
        out_specs=P(("seq", "kvh"), None),
        check_vma=False,
    )
```

```python
import functools
import math

import jax
import jax.numpy as jnp
from jax import lax
from jax.experimental import pallas as pl
from jax.experimental.pallas import tpu as pltpu
from jax.sharding import PartitionSpec as P

DH = 128
BUNCH = 4


def shifted(block, axis, distance):
    devices = range(lax.axis_size(axis))
    route = [(i - distance, i) for i in devices if i - distance in devices]
    return lax.ppermute(block, axis, route)


def doc_start(position, doc_ends, doc_lengths):
    return jnp.sum(
        jnp.where(doc_ends[None, :] <= position[:, None], doc_lengths[None, :], 0), axis=1
    )


def attend_kernel(
    blocks_ref, q_ref, start_ref, *refs, half_rows, group_size, pad_rows, window, kv_feat
):
    pieces = window // half_rows
    low_refs = refs[:pieces]
    high_refs = refs[pieces : 2 * pieces]
    out_ref, kt_buf, v_buf = refs[2 * pieces :]
    side = pl.program_id(0)
    head = pl.program_id(1)
    block_id = blocks_ref[side]
    needed = blocks_ref[2 + side]
    k_lanes = pl.ds(pl.multiple_of(head * DH, DH), DH)
    v_lanes = pl.ds(pl.multiple_of(kv_feat + head * DH, DH), DH)
    for piece_no in range(pieces):
        keys_at = slice(piece_no * half_rows, (piece_no + 1) * half_rows)
        for side_no, piece_refs in enumerate((low_refs, high_refs)):

            @pl.when(side == side_no)
            def _(piece_ref=piece_refs[piece_no], keys_at=keys_at):
                kt_buf[:, keys_at] = piece_ref[:, k_lanes].T
                v_buf[keys_at, :DH] = piece_ref[:, v_lanes]

    lane = lax.broadcasted_iota(jnp.int32, (window, DH), 1)
    v_buf[:, DH:] = jnp.where(lane == 0, 1.0, 0.0).astype(v_buf.dtype)
    scale = 1.0 / math.sqrt(DH)
    row_start = start_ref[...]

    def dense(span):
        skip = window - span
        row_pos = block_id * half_rows + lax.broadcasted_iota(jnp.int32, (half_rows, span), 0)
        key_pos = block_id * half_rows - pad_rows + skip + lax.broadcasted_iota(
            jnp.int32, (half_rows, span), 1
        )
        allowed = (key_pos <= row_pos) & (key_pos >= row_start)
        bias = jnp.where(allowed, 0.0, -jnp.inf).astype(jnp.float32)

        def one_pair(pair, carry):
            cols = [pl.multiple_of((BUNCH * pair + i) * DH, DH) for i in range(BUNCH)]
            q_two = jnp.concatenate([q_ref[:, pl.ds(c, DH)] for c in cols], axis=0)
            scores = jnp.dot(q_two, kt_buf[:, skip:], preferred_element_type=jnp.float32)
            scores = scores.reshape(BUNCH, half_rows, span) * scale + bias[None]
            top = jnp.max(scores, axis=2, keepdims=True)
            weights = jnp.exp(scores - top).reshape(BUNCH * half_rows, span)
            mixed = jnp.dot(
                weights.astype(jnp.bfloat16), v_buf[skip:, :], preferred_element_type=jnp.float32
            )
            normed = mixed[:, :DH] / mixed[:, DH : DH + 1]
            for i in range(BUNCH):
                out_ref[:, pl.ds(cols[i], DH)] = normed[i * half_rows : (i + 1) * half_rows].astype(
                    out_ref.dtype
                )
            return carry

        lax.fori_loop(0, group_size // BUNCH, one_pair, 0, unroll=True)

    for count in range(1, window // half_rows + 1):

        @pl.when(needed == count)
        def _(count=count):
            dense(count * half_rows)


def on_device(queries, key_rows, value_rows, doc_lengths):
    shards = lax.axis_size("seq")
    kvh = lax.axis_size("kvh")
    my_shard = lax.axis_index("seq")
    rows_in = key_rows.shape[0]
    head_queries = lax.all_to_all(queries, "kvh", split_axis=1, concat_axis=0, tiled=True)
    kv_cols = key_rows.shape[1] // kvh
    kv_local = jnp.concatenate(
        [key_rows.reshape(rows_in, kvh, kv_cols), value_rows.reshape(rows_in, kvh, kv_cols)],
        axis=2,
    )
    kv_slab = lax.all_to_all(kv_local, "kvh", split_axis=1, concat_axis=0, tiled=True)
    dev_rows = kv_slab.shape[0]
    kv_slab = kv_slab.reshape(dev_rows, 2 * kv_cols)
    half_rows = dev_rows // 2
    kv_feat = kv_cols
    kv_heads = kv_feat // DH
    group_size = head_queries.shape[1] // kv_feat
    seq_total = dev_rows * shards
    longest = min(13 * half_rows, seq_total // 4)
    lookback = (longest + half_rows - 2) // half_rows
    pad_rows = lookback * half_rows
    window = pad_rows + half_rows

    first_half = kv_slab[:half_rows]
    second_half = kv_slab[half_rows:]
    blank = jnp.zeros_like(first_half)
    low_side = [first_half]
    high_side = [second_half]
    for back in range(1, lookback + 1):
        from_low = shifted(first_half, "seq", back)
        from_high = shifted(second_half, "seq", -back)
        mirror = [(t, 2 * shards - 1 - back - t) for t in range(shards)]
        mirror = [(t, u) for t, u in mirror if 0 <= u < shards and u != t]
        from_mirror = lax.ppermute(first_half, "seq", mirror) if mirror else blank
        wanted = 2 * shards - 1 - my_shard - back
        high_pick = jnp.where(
            wanted >= shards, from_high, jnp.where(wanted == my_shard, first_half, from_mirror)
        )
        low_side.append(from_low)
        high_side.append(high_pick)
    pieces = low_side[::-1] + high_side[::-1]

    doc_ends = jnp.cumsum(doc_lengths)
    block_ids = jnp.stack([my_shard, 2 * shards - 1 - my_shard]).astype(jnp.int32)
    positions = block_ids[:, None] * half_rows + jnp.arange(half_rows, dtype=jnp.int32)[None, :]
    starts = doc_start(positions.reshape(-1), doc_ends, doc_lengths).astype(jnp.int32)
    needed = 1 + jnp.clip((block_ids * half_rows - starts[::half_rows] + half_rows - 1) // half_rows, 0, lookback)
    block_ids = jnp.concatenate([block_ids, needed.astype(jnp.int32)])
    starts = starts.reshape(2, half_rows, 1)

    kernel = functools.partial(
        attend_kernel,
        half_rows=half_rows,
        group_size=group_size,
        pad_rows=pad_rows,
        window=window,
        kv_feat=kv_feat,
    )
    q_cols = group_size * DH
    merged = pl.pallas_call(
        kernel,
        out_shape=jax.ShapeDtypeStruct(head_queries.shape, head_queries.dtype),
        grid_spec=pltpu.PrefetchScalarGridSpec(
            num_scalar_prefetch=1,
            grid=(2, kv_heads),
            in_specs=[
                pl.BlockSpec((half_rows, q_cols), lambda s, h, b: (s, h)),
                pl.BlockSpec((None, half_rows, 1), lambda s, h, b: (s, 0, 0)),
            ]
            + [pl.BlockSpec((half_rows, 2 * kv_feat), lambda s, h, b: (0, 0))] * len(pieces),
            out_specs=pl.BlockSpec((half_rows, q_cols), lambda s, h, b: (s, h)),
            scratch_shapes=[
                pltpu.VMEM((DH, window), kv_slab.dtype),
                pltpu.VMEM((window, 2 * DH), kv_slab.dtype),
            ],
        ),
    )(block_ids, head_queries, starts, *pieces)
    return lax.all_to_all(merged, "kvh", split_axis=0, concat_axis=1, tiled=True)


def solution(mesh):
    return jax.shard_map(
        on_device,
        mesh=mesh,
        in_specs=(P(("seq", "kvh"), None), P(("seq", "kvh"), None), P(("seq", "kvh"), None), P()),
        out_specs=P(("seq", "kvh"), None),
        check_vma=False,
    )
```

```python
import functools
import math

import jax
import jax.numpy as jnp
from jax import lax
from jax.experimental import pallas as pl
from jax.experimental.pallas import tpu as pltpu
from jax.sharding import PartitionSpec as P

DH = 128
BUNCH = 4


def shifted(block, axis, distance):
    devices = range(lax.axis_size(axis))
    route = [(i - distance, i) for i in devices if i - distance in devices]
    return lax.ppermute(block, axis, route)


def doc_start(position, doc_ends, doc_lengths):
    return jnp.sum(
        jnp.where(doc_ends[None, :] <= position[:, None], doc_lengths[None, :], 0), axis=1
    )


def attend_kernel(
    blocks_ref, q_ref, start_ref, *refs, half_rows, group_size, pad_rows, window, kv_feat
):
    pieces = window // half_rows
    low_refs = refs[:pieces]
    high_refs = refs[pieces : 2 * pieces]
    out_ref, kt_buf, v_buf = refs[2 * pieces :]
    side = pl.program_id(0)
    head = pl.program_id(1)
    block_id = blocks_ref[side]
    needed = blocks_ref[2 + side]
    k_lanes = pl.ds(pl.multiple_of(head * DH, DH), DH)
    v_lanes = pl.ds(pl.multiple_of(kv_feat + head * DH, DH), DH)
    for piece_no in range(pieces):
        keys_at = slice(piece_no * half_rows, (piece_no + 1) * half_rows)
        for side_no, piece_refs in enumerate((low_refs, high_refs)):

            @pl.when((side == side_no) & (piece_no >= pieces - needed))
            def _(piece_ref=piece_refs[piece_no], keys_at=keys_at):
                kt_buf[:, keys_at] = piece_ref[:, k_lanes].T
                v_buf[keys_at, :DH] = piece_ref[:, v_lanes]

    lane = lax.broadcasted_iota(jnp.int32, (window, DH), 1)
    v_buf[:, DH:] = jnp.where(lane == 0, 1.0, 0.0).astype(v_buf.dtype)
    scale = 1.0 / math.sqrt(DH)
    row_start = start_ref[...]

    def dense(span):
        skip = window - span
        row_pos = block_id * half_rows + lax.broadcasted_iota(jnp.int32, (half_rows, span), 0)
        key_pos = block_id * half_rows - pad_rows + skip + lax.broadcasted_iota(
            jnp.int32, (half_rows, span), 1
        )
        allowed = (key_pos <= row_pos) & (key_pos >= row_start)
        bias = jnp.where(allowed, 0.0, -jnp.inf).astype(jnp.float32)

        def one_pair(pair, carry):
            cols = [pl.multiple_of((BUNCH * pair + i) * DH, DH) for i in range(BUNCH)]
            q_two = jnp.concatenate([q_ref[:, pl.ds(c, DH)] for c in cols], axis=0)
            scores = jnp.dot(q_two, kt_buf[:, skip:], preferred_element_type=jnp.float32)
            scores = scores.reshape(BUNCH, half_rows, span) * scale + bias[None]
            top = jnp.max(scores, axis=2, keepdims=True)
            weights = jnp.exp(scores - top).reshape(BUNCH * half_rows, span)
            mixed = jnp.dot(
                weights.astype(jnp.bfloat16), v_buf[skip:, :], preferred_element_type=jnp.float32
            )
            normed = mixed[:, :DH] / mixed[:, DH : DH + 1]
            for i in range(BUNCH):
                out_ref[:, pl.ds(cols[i], DH)] = normed[i * half_rows : (i + 1) * half_rows].astype(
                    out_ref.dtype
                )
            return carry

        lax.fori_loop(0, group_size // BUNCH, one_pair, 0, unroll=True)

    for count in range(1, window // half_rows + 1):

        @pl.when(needed == count)
        def _(count=count):
            dense(count * half_rows)


def on_device(queries, key_rows, value_rows, doc_lengths):
    shards = lax.axis_size("seq")
    kvh = lax.axis_size("kvh")
    my_shard = lax.axis_index("seq")
    rows_in = key_rows.shape[0]
    head_queries = lax.all_to_all(queries, "kvh", split_axis=1, concat_axis=0, tiled=True)
    kv_cols = key_rows.shape[1] // kvh
    kv_local = jnp.concatenate(
        [key_rows.reshape(rows_in, kvh, kv_cols), value_rows.reshape(rows_in, kvh, kv_cols)],
        axis=2,
    )
    kv_slab = lax.all_to_all(kv_local, "kvh", split_axis=1, concat_axis=0, tiled=True)
    dev_rows = kv_slab.shape[0]
    kv_slab = kv_slab.reshape(dev_rows, 2 * kv_cols)
    half_rows = dev_rows // 2
    kv_feat = kv_cols
    kv_heads = kv_feat // DH
    group_size = head_queries.shape[1] // kv_feat
    seq_total = dev_rows * shards
    longest = min(13 * half_rows, seq_total // 4)
    lookback = (longest + half_rows - 2) // half_rows
    pad_rows = lookback * half_rows
    window = pad_rows + half_rows

    first_half = kv_slab[:half_rows]
    second_half = kv_slab[half_rows:]
    blank = jnp.zeros_like(first_half)
    low_side = [first_half]
    high_side = [second_half]
    for back in range(1, lookback + 1):
        from_low = shifted(first_half, "seq", back)
        from_high = shifted(second_half, "seq", -back)
        mirror = [(t, 2 * shards - 1 - back - t) for t in range(shards)]
        mirror = [(t, u) for t, u in mirror if 0 <= u < shards and u != t]
        from_mirror = lax.ppermute(first_half, "seq", mirror) if mirror else blank
        wanted = 2 * shards - 1 - my_shard - back
        high_pick = jnp.where(
            wanted >= shards, from_high, jnp.where(wanted == my_shard, first_half, from_mirror)
        )
        low_side.append(from_low)
        high_side.append(high_pick)
    pieces = low_side[::-1] + high_side[::-1]

    doc_ends = jnp.cumsum(doc_lengths)
    block_ids = jnp.stack([my_shard, 2 * shards - 1 - my_shard]).astype(jnp.int32)
    positions = block_ids[:, None] * half_rows + jnp.arange(half_rows, dtype=jnp.int32)[None, :]
    starts = doc_start(positions.reshape(-1), doc_ends, doc_lengths).astype(jnp.int32)
    needed = 1 + jnp.clip((block_ids * half_rows - starts[::half_rows] + half_rows - 1) // half_rows, 0, lookback)
    block_ids = jnp.concatenate([block_ids, needed.astype(jnp.int32)])
    starts = starts.reshape(2, half_rows, 1)

    kernel = functools.partial(
        attend_kernel,
        half_rows=half_rows,
        group_size=group_size,
        pad_rows=pad_rows,
        window=window,
        kv_feat=kv_feat,
    )
    q_cols = group_size * DH
    merged = pl.pallas_call(
        kernel,
        out_shape=jax.ShapeDtypeStruct(head_queries.shape, head_queries.dtype),
        grid_spec=pltpu.PrefetchScalarGridSpec(
            num_scalar_prefetch=1,
            grid=(2, kv_heads),
            in_specs=[
                pl.BlockSpec((half_rows, q_cols), lambda s, h, b: (s, h)),
                pl.BlockSpec((None, half_rows, 1), lambda s, h, b: (s, 0, 0)),
            ]
            + [pl.BlockSpec((half_rows, 2 * kv_feat), lambda s, h, b: (0, 0))] * len(pieces),
            out_specs=pl.BlockSpec((half_rows, q_cols), lambda s, h, b: (s, h)),
            scratch_shapes=[
                pltpu.VMEM((DH, window), kv_slab.dtype),
                pltpu.VMEM((window, 2 * DH), kv_slab.dtype),
            ],
        ),
    )(block_ids, head_queries, starts, *pieces)
    return lax.all_to_all(merged, "kvh", split_axis=0, concat_axis=1, tiled=True)


def solution(mesh):
    return jax.shard_map(
        on_device,
        mesh=mesh,
        in_specs=(P(("seq", "kvh"), None), P(("seq", "kvh"), None), P(("seq", "kvh"), None), P()),
        out_specs=P(("seq", "kvh"), None),
        check_vma=False,
    )
```

```python
import functools
import math

import jax
import jax.numpy as jnp
from jax import lax
from jax.experimental import pallas as pl
from jax.experimental.pallas import tpu as pltpu
from jax.sharding import PartitionSpec as P

DH = 128
BUNCH = 4


def shifted(block, axis, distance):
    devices = range(lax.axis_size(axis))
    route = [(i - distance, i) for i in devices if i - distance in devices]
    return lax.ppermute(block, axis, route)


def doc_start(position, doc_ends, doc_lengths):
    return jnp.sum(
        jnp.where(doc_ends[None, :] <= position[:, None], doc_lengths[None, :], 0), axis=1
    )


def attend_kernel(
    blocks_ref, q_ref, start_ref, *refs, half_rows, group_size, pad_rows, window, kv_feat
):
    pieces = window // half_rows
    low_refs = refs[:pieces]
    high_refs = refs[pieces : 3 * pieces - 1]
    out_ref, kt_buf, v_buf = refs[3 * pieces - 1 :]
    side = pl.program_id(0)
    head = pl.program_id(1)
    block_id = blocks_ref[side]
    needed = blocks_ref[2 + side]
    k_lanes = pl.ds(pl.multiple_of(head * DH, DH), DH)
    v_lanes = pl.ds(pl.multiple_of(kv_feat + head * DH, DH), DH)

    def fill(piece_ref, keys_at):
        kt_buf[:, keys_at] = piece_ref[:, k_lanes].T
        v_buf[keys_at, :DH] = piece_ref[:, v_lanes]

    for piece_no in range(pieces):
        keys_at = slice(piece_no * half_rows, (piece_no + 1) * half_rows)
        back = pieces - 1 - piece_no
        pl.when(side == 0)(functools.partial(fill, low_refs[piece_no], keys_at))
        if back == 0:
            pl.when(side == 1)(functools.partial(fill, high_refs[0], keys_at))
            continue
        source = blocks_ref[3 + back]
        choices = (high_refs[2 * back - 1], low_refs[pieces - 1], high_refs[2 * back])
        for code, piece_ref in enumerate(choices):
            pl.when((side == 1) & (source == code))(functools.partial(fill, piece_ref, keys_at))

    lane = lax.broadcasted_iota(jnp.int32, (window, DH), 1)
    v_buf[:, DH:] = jnp.where(lane == 0, 1.0, 0.0).astype(v_buf.dtype)
    scale = 1.0 / math.sqrt(DH)
    row_start = start_ref[...]

    def dense(span):
        skip = window - span
        row_pos = block_id * half_rows + lax.broadcasted_iota(jnp.int32, (half_rows, span), 0)
        key_pos = block_id * half_rows - pad_rows + skip + lax.broadcasted_iota(
            jnp.int32, (half_rows, span), 1
        )
        allowed = (key_pos <= row_pos) & (key_pos >= row_start)
        bias = jnp.where(allowed, 0.0, -jnp.inf).astype(jnp.float32)

        def one_pair(pair, carry):
            cols = [pl.multiple_of((BUNCH * pair + i) * DH, DH) for i in range(BUNCH)]
            q_two = jnp.concatenate([q_ref[:, pl.ds(c, DH)] for c in cols], axis=0)
            scores = jnp.dot(q_two, kt_buf[:, skip:], preferred_element_type=jnp.float32)
            scores = scores.reshape(BUNCH, half_rows, span) * scale + bias[None]
            top = jnp.max(scores, axis=2, keepdims=True)
            weights = jnp.exp(scores - top).reshape(BUNCH * half_rows, span)
            mixed = jnp.dot(
                weights.astype(jnp.bfloat16), v_buf[skip:, :], preferred_element_type=jnp.float32
            )
            normed = mixed[:, :DH] / mixed[:, DH : DH + 1]
            for i in range(BUNCH):
                out_ref[:, pl.ds(cols[i], DH)] = normed[i * half_rows : (i + 1) * half_rows].astype(
                    out_ref.dtype
                )
            return carry

        lax.fori_loop(0, group_size // BUNCH, one_pair, 0, unroll=True)

    for count in range(1, window // half_rows + 1):

        @pl.when(needed == count)
        def _(count=count):
            dense(count * half_rows)


def on_device(queries, key_rows, value_rows, doc_lengths):
    shards = lax.axis_size("seq")
    kvh = lax.axis_size("kvh")
    my_shard = lax.axis_index("seq")
    rows_in = key_rows.shape[0]
    head_queries = lax.all_to_all(queries, "kvh", split_axis=1, concat_axis=0, tiled=True)
    kv_cols = key_rows.shape[1] // kvh
    kv_local = jnp.concatenate(
        [key_rows.reshape(rows_in, kvh, kv_cols), value_rows.reshape(rows_in, kvh, kv_cols)],
        axis=2,
    )
    kv_slab = lax.all_to_all(kv_local, "kvh", split_axis=1, concat_axis=0, tiled=True)
    dev_rows = kv_slab.shape[0]
    kv_slab = kv_slab.reshape(dev_rows, 2 * kv_cols)
    half_rows = dev_rows // 2
    kv_feat = kv_cols
    kv_heads = kv_feat // DH
    group_size = head_queries.shape[1] // kv_feat
    seq_total = dev_rows * shards
    longest = min(13 * half_rows, seq_total // 4)
    lookback = (longest + half_rows - 2) // half_rows
    pad_rows = lookback * half_rows
    window = pad_rows + half_rows

    first_half = kv_slab[:half_rows]
    second_half = kv_slab[half_rows:]
    blank = jnp.zeros_like(first_half)
    low_side = [first_half]
    high_side = [second_half]
    sources = []
    for back in range(1, lookback + 1):
        from_low = shifted(first_half, "seq", back)
        from_high = shifted(second_half, "seq", -back)
        mirror = [(t, 2 * shards - 1 - back - t) for t in range(shards)]
        mirror = [(t, u) for t, u in mirror if 0 <= u < shards and u != t]
        from_mirror = lax.ppermute(first_half, "seq", mirror) if mirror else blank
        wanted = 2 * shards - 1 - my_shard - back
        source = jnp.where(wanted >= shards, 0, jnp.where(wanted == my_shard, 1, 2))
        low_side.append(from_low)
        high_side.append((from_high, from_mirror))
        sources.append(source)
    pieces = low_side[::-1] + [second_half] + [p for pair in high_side[1:] for p in pair]

    doc_ends = jnp.cumsum(doc_lengths)
    block_ids = jnp.stack([my_shard, 2 * shards - 1 - my_shard]).astype(jnp.int32)
    positions = block_ids[:, None] * half_rows + jnp.arange(half_rows, dtype=jnp.int32)[None, :]
    starts = doc_start(positions.reshape(-1), doc_ends, doc_lengths).astype(jnp.int32)
    needed = 1 + jnp.clip((block_ids * half_rows - starts[::half_rows] + half_rows - 1) // half_rows, 0, lookback)
    block_ids = jnp.concatenate([block_ids, needed.astype(jnp.int32), jnp.stack(sources).astype(jnp.int32)])
    starts = starts.reshape(2, half_rows, 1)

    kernel = functools.partial(
        attend_kernel,
        half_rows=half_rows,
        group_size=group_size,
        pad_rows=pad_rows,
        window=window,
        kv_feat=kv_feat,
    )
    q_cols = group_size * DH
    merged = pl.pallas_call(
        kernel,
        out_shape=jax.ShapeDtypeStruct(head_queries.shape, head_queries.dtype),
        grid_spec=pltpu.PrefetchScalarGridSpec(
            num_scalar_prefetch=1,
            grid=(2, kv_heads),
            in_specs=[
                pl.BlockSpec((half_rows, q_cols), lambda s, h, b: (s, h)),
                pl.BlockSpec((None, half_rows, 1), lambda s, h, b: (s, 0, 0)),
            ]
            + [pl.BlockSpec((half_rows, 2 * kv_feat), lambda s, h, b: (0, 0))] * len(pieces),
            out_specs=pl.BlockSpec((half_rows, q_cols), lambda s, h, b: (s, h)),
            scratch_shapes=[
                pltpu.VMEM((DH, window), kv_slab.dtype),
                pltpu.VMEM((window, 2 * DH), kv_slab.dtype),
            ],
        ),
    )(block_ids, head_queries, starts, *pieces)
    return lax.all_to_all(merged, "kvh", split_axis=0, concat_axis=1, tiled=True)


def solution(mesh):
    return jax.shard_map(
        on_device,
        mesh=mesh,
        in_specs=(P(("seq", "kvh"), None), P(("seq", "kvh"), None), P(("seq", "kvh"), None), P()),
        out_specs=P(("seq", "kvh"), None),
        check_vma=False,
    )
```

```python
import functools
import math

import jax
import jax.numpy as jnp
from jax import lax
from jax.experimental import pallas as pl
from jax.experimental.pallas import tpu as pltpu
from jax.sharding import PartitionSpec as P

DH = 128
BUNCH = 8


def shifted(block, axis, distance):
    devices = range(lax.axis_size(axis))
    route = [(i - distance, i) for i in devices if i - distance in devices]
    return lax.ppermute(block, axis, route)


def doc_start(position, doc_ends, doc_lengths):
    return jnp.sum(
        jnp.where(doc_ends[None, :] <= position[:, None], doc_lengths[None, :], 0), axis=1
    )


def attend_kernel(
    blocks_ref, q_ref, start_ref, *refs, half_rows, group_size, pad_rows, window, kv_feat
):
    pieces = window // half_rows
    low_refs = refs[:pieces]
    high_refs = refs[pieces : 2 * pieces]
    out_ref, kt_buf, v_buf = refs[2 * pieces :]
    side = pl.program_id(0)
    head = pl.program_id(1)
    block_id = blocks_ref[side]
    needed = blocks_ref[2 + side]
    k_lanes = pl.ds(pl.multiple_of(head * DH, DH), DH)
    v_lanes = pl.ds(pl.multiple_of(kv_feat + head * DH, DH), DH)
    for piece_no in range(pieces):
        keys_at = slice(piece_no * half_rows, (piece_no + 1) * half_rows)
        for side_no, piece_refs in enumerate((low_refs, high_refs)):

            @pl.when(side == side_no)
            def _(piece_ref=piece_refs[piece_no], keys_at=keys_at):
                kt_buf[:, keys_at] = piece_ref[:, k_lanes].T
                v_buf[keys_at, :DH] = piece_ref[:, v_lanes]

    lane = lax.broadcasted_iota(jnp.int32, (window, DH), 1)
    v_buf[:, DH:] = jnp.where(lane == 0, 1.0, 0.0).astype(v_buf.dtype)
    scale = 1.0 / math.sqrt(DH)
    row_start = start_ref[...]

    def dense(span):
        skip = window - span
        row_pos = block_id * half_rows + lax.broadcasted_iota(jnp.int32, (half_rows, span), 0)
        key_pos = block_id * half_rows - pad_rows + skip + lax.broadcasted_iota(
            jnp.int32, (half_rows, span), 1
        )
        allowed = (key_pos <= row_pos) & (key_pos >= row_start)
        bias = jnp.where(allowed, 0.0, -jnp.inf).astype(jnp.float32)

        def one_pair(pair, carry):
            cols = [pl.multiple_of((BUNCH * pair + i) * DH, DH) for i in range(BUNCH)]
            q_two = jnp.concatenate([q_ref[:, pl.ds(c, DH)] for c in cols], axis=0)
            scores = jnp.dot(q_two, kt_buf[:, skip:], preferred_element_type=jnp.float32)
            scores = scores.reshape(BUNCH, half_rows, span) * scale + bias[None]
            top = jnp.max(scores, axis=2, keepdims=True)
            weights = jnp.exp(scores - top).reshape(BUNCH * half_rows, span)
            mixed = jnp.dot(
                weights.astype(jnp.bfloat16), v_buf[skip:, :], preferred_element_type=jnp.float32
            )
            normed = mixed[:, :DH] / mixed[:, DH : DH + 1]
            for i in range(BUNCH):
                out_ref[:, pl.ds(cols[i], DH)] = normed[i * half_rows : (i + 1) * half_rows].astype(
                    out_ref.dtype
                )
            return carry

        lax.fori_loop(0, group_size // BUNCH, one_pair, 0, unroll=True)

    for count in range(1, window // half_rows + 1):

        @pl.when(needed == count)
        def _(count=count):
            dense(count * half_rows)


def on_device(queries, key_rows, value_rows, doc_lengths):
    shards = lax.axis_size("seq")
    kvh = lax.axis_size("kvh")
    my_shard = lax.axis_index("seq")
    rows_in = key_rows.shape[0]
    head_queries = lax.all_to_all(queries, "kvh", split_axis=1, concat_axis=0, tiled=True)
    kv_cols = key_rows.shape[1] // kvh
    kv_local = jnp.concatenate(
        [key_rows.reshape(rows_in, kvh, kv_cols), value_rows.reshape(rows_in, kvh, kv_cols)],
        axis=2,
    )
    kv_slab = lax.all_to_all(kv_local, "kvh", split_axis=1, concat_axis=0, tiled=True)
    dev_rows = kv_slab.shape[0]
    kv_slab = kv_slab.reshape(dev_rows, 2 * kv_cols)
    half_rows = dev_rows // 2
    kv_feat = kv_cols
    kv_heads = kv_feat // DH
    group_size = head_queries.shape[1] // kv_feat
    seq_total = dev_rows * shards
    longest = min(13 * half_rows, seq_total // 4)
    lookback = (longest + half_rows - 2) // half_rows
    pad_rows = lookback * half_rows
    window = pad_rows + half_rows

    first_half = kv_slab[:half_rows]
    second_half = kv_slab[half_rows:]
    blank = jnp.zeros_like(first_half)
    low_side = [first_half]
    high_side = [second_half]
    for back in range(1, lookback + 1):
        from_low = shifted(first_half, "seq", back)
        from_high = shifted(second_half, "seq", -back)
        mirror = [(t, 2 * shards - 1 - back - t) for t in range(shards)]
        mirror = [(t, u) for t, u in mirror if 0 <= u < shards and u != t]
        from_mirror = lax.ppermute(first_half, "seq", mirror) if mirror else blank
        wanted = 2 * shards - 1 - my_shard - back
        high_pick = jnp.where(
            wanted >= shards, from_high, jnp.where(wanted == my_shard, first_half, from_mirror)
        )
        low_side.append(from_low)
        high_side.append(high_pick)
    pieces = low_side[::-1] + high_side[::-1]

    doc_ends = jnp.cumsum(doc_lengths)
    block_ids = jnp.stack([my_shard, 2 * shards - 1 - my_shard]).astype(jnp.int32)
    positions = block_ids[:, None] * half_rows + jnp.arange(half_rows, dtype=jnp.int32)[None, :]
    starts = doc_start(positions.reshape(-1), doc_ends, doc_lengths).astype(jnp.int32)
    needed = 1 + jnp.clip((block_ids * half_rows - starts[::half_rows] + half_rows - 1) // half_rows, 0, lookback)
    block_ids = jnp.concatenate([block_ids, needed.astype(jnp.int32)])
    starts = starts.reshape(2, half_rows, 1)

    kernel = functools.partial(
        attend_kernel,
        half_rows=half_rows,
        group_size=group_size,
        pad_rows=pad_rows,
        window=window,
        kv_feat=kv_feat,
    )
    q_cols = group_size * DH
    merged = pl.pallas_call(
        kernel,
        out_shape=jax.ShapeDtypeStruct(head_queries.shape, head_queries.dtype),
        grid_spec=pltpu.PrefetchScalarGridSpec(
            num_scalar_prefetch=1,
            grid=(2, kv_heads),
            in_specs=[
                pl.BlockSpec((half_rows, q_cols), lambda s, h, b: (s, h)),
                pl.BlockSpec((None, half_rows, 1), lambda s, h, b: (s, 0, 0)),
            ]
            + [pl.BlockSpec((half_rows, 2 * kv_feat), lambda s, h, b: (0, 0))] * len(pieces),
            out_specs=pl.BlockSpec((half_rows, q_cols), lambda s, h, b: (s, h)),
            scratch_shapes=[
                pltpu.VMEM((DH, window), kv_slab.dtype),
                pltpu.VMEM((window, 2 * DH), kv_slab.dtype),
            ],
        ),
    )(block_ids, head_queries, starts, *pieces)
    return lax.all_to_all(merged, "kvh", split_axis=0, concat_axis=1, tiled=True)


def solution(mesh):
    return jax.shard_map(
        on_device,
        mesh=mesh,
        in_specs=(P(("seq", "kvh"), None), P(("seq", "kvh"), None), P(("seq", "kvh"), None), P()),
        out_specs=P(("seq", "kvh"), None),
        check_vma=False,
    )
```

```python
import functools
import math

import jax
import jax.numpy as jnp
from jax import lax
from jax.experimental import pallas as pl
from jax.experimental.pallas import tpu as pltpu
from jax.sharding import PartitionSpec as P

DH = 128
BUNCH = 4


def shifted(block, axis, distance):
    devices = range(lax.axis_size(axis))
    route = [(i - distance, i) for i in devices if i - distance in devices]
    return lax.ppermute(block, axis, route)


def doc_start(position, doc_ends, doc_lengths):
    return jnp.sum(
        jnp.where(doc_ends[None, :] <= position[:, None], doc_lengths[None, :], 0), axis=1
    )


def attend_kernel(
    blocks_ref, q_ref, start_ref, *refs, half_rows, group_size, pad_rows, window, kv_feat
):
    pieces = window // half_rows
    low_refs = refs[:pieces]
    high_refs = refs[pieces : 2 * pieces]
    out_ref, kt_buf, v_buf = refs[2 * pieces :]
    side = pl.program_id(0)
    head = pl.program_id(1)
    block_id = blocks_ref[side]
    needed = blocks_ref[2 + side]
    k_lanes = pl.ds(pl.multiple_of(head * DH, DH), DH)
    v_lanes = pl.ds(pl.multiple_of(kv_feat + head * DH, DH), DH)
    for piece_no in range(pieces):
        keys_at = slice(piece_no * half_rows, (piece_no + 1) * half_rows)
        for side_no, piece_refs in enumerate((low_refs, high_refs)):

            @pl.when(side == side_no)
            def _(piece_ref=piece_refs[piece_no], keys_at=keys_at):
                kt_buf[:, keys_at] = piece_ref[:, k_lanes].T
                v_buf[keys_at, :DH] = piece_ref[:, v_lanes]

    @pl.when((side == 0) & (head == 0))
    def _():
        lane = lax.broadcasted_iota(jnp.int32, (window, DH), 1)
        v_buf[:, DH:] = jnp.where(lane == 0, 1.0, 0.0).astype(v_buf.dtype)

    scale = 1.0 / math.sqrt(DH)
    row_start = start_ref[...]

    def dense(span):
        skip = window - span
        row_pos = block_id * half_rows + lax.broadcasted_iota(jnp.int32, (half_rows, span), 0)
        key_pos = block_id * half_rows - pad_rows + skip + lax.broadcasted_iota(
            jnp.int32, (half_rows, span), 1
        )
        allowed = (key_pos <= row_pos) & (key_pos >= row_start)
        bias = jnp.where(allowed, 0.0, -jnp.inf).astype(jnp.float32)

        def one_pair(pair, carry):
            cols = [pl.multiple_of((BUNCH * pair + i) * DH, DH) for i in range(BUNCH)]
            q_two = jnp.concatenate([q_ref[:, pl.ds(c, DH)] for c in cols], axis=0)
            scores = jnp.dot(q_two, kt_buf[:, skip:], preferred_element_type=jnp.float32)
            scores = scores.reshape(BUNCH, half_rows, span) * scale + bias[None]
            top = jnp.max(scores, axis=2, keepdims=True)
            weights = jnp.exp(scores - top).reshape(BUNCH * half_rows, span)
            mixed = jnp.dot(
                weights.astype(jnp.bfloat16), v_buf[skip:, :], preferred_element_type=jnp.float32
            )
            normed = mixed[:, :DH] / mixed[:, DH : DH + 1]
            for i in range(BUNCH):
                out_ref[:, pl.ds(cols[i], DH)] = normed[i * half_rows : (i + 1) * half_rows].astype(
                    out_ref.dtype
                )
            return carry

        lax.fori_loop(0, group_size // BUNCH, one_pair, 0, unroll=True)

    for count in range(1, window // half_rows + 1):

        @pl.when(needed == count)
        def _(count=count):
            dense(count * half_rows)


def on_device(queries, key_rows, value_rows, doc_lengths):
    shards = lax.axis_size("seq")
    kvh = lax.axis_size("kvh")
    my_shard = lax.axis_index("seq")
    rows_in = key_rows.shape[0]
    head_queries = lax.all_to_all(queries, "kvh", split_axis=1, concat_axis=0, tiled=True)
    kv_cols = key_rows.shape[1] // kvh
    kv_local = jnp.concatenate(
        [key_rows.reshape(rows_in, kvh, kv_cols), value_rows.reshape(rows_in, kvh, kv_cols)],
        axis=2,
    )
    kv_slab = lax.all_to_all(kv_local, "kvh", split_axis=1, concat_axis=0, tiled=True)
    dev_rows = kv_slab.shape[0]
    kv_slab = kv_slab.reshape(dev_rows, 2 * kv_cols)
    half_rows = dev_rows // 2
    kv_feat = kv_cols
    kv_heads = kv_feat // DH
    group_size = head_queries.shape[1] // kv_feat
    seq_total = dev_rows * shards
    longest = min(13 * half_rows, seq_total // 4)
    lookback = (longest + half_rows - 2) // half_rows
    pad_rows = lookback * half_rows
    window = pad_rows + half_rows

    first_half = kv_slab[:half_rows]
    second_half = kv_slab[half_rows:]
    blank = jnp.zeros_like(first_half)
    low_side = [first_half]
    high_side = [second_half]
    for back in range(1, lookback + 1):
        from_low = shifted(first_half, "seq", back)
        from_high = shifted(second_half, "seq", -back)
        mirror = [(t, 2 * shards - 1 - back - t) for t in range(shards)]
        mirror = [(t, u) for t, u in mirror if 0 <= u < shards and u != t]
        from_mirror = lax.ppermute(first_half, "seq", mirror) if mirror else blank
        wanted = 2 * shards - 1 - my_shard - back
        high_pick = jnp.where(
            wanted >= shards, from_high, jnp.where(wanted == my_shard, first_half, from_mirror)
        )
        low_side.append(from_low)
        high_side.append(high_pick)
    pieces = low_side[::-1] + high_side[::-1]

    doc_ends = jnp.cumsum(doc_lengths)
    block_ids = jnp.stack([my_shard, 2 * shards - 1 - my_shard]).astype(jnp.int32)
    positions = block_ids[:, None] * half_rows + jnp.arange(half_rows, dtype=jnp.int32)[None, :]
    starts = doc_start(positions.reshape(-1), doc_ends, doc_lengths).astype(jnp.int32)
    needed = 1 + jnp.clip((block_ids * half_rows - starts[::half_rows] + half_rows - 1) // half_rows, 0, lookback)
    block_ids = jnp.concatenate([block_ids, needed.astype(jnp.int32)])
    starts = starts.reshape(2, half_rows, 1)

    kernel = functools.partial(
        attend_kernel,
        half_rows=half_rows,
        group_size=group_size,
        pad_rows=pad_rows,
        window=window,
        kv_feat=kv_feat,
    )
    q_cols = group_size * DH
    merged = pl.pallas_call(
        kernel,
        out_shape=jax.ShapeDtypeStruct(head_queries.shape, head_queries.dtype),
        grid_spec=pltpu.PrefetchScalarGridSpec(
            num_scalar_prefetch=1,
            grid=(2, kv_heads),
            in_specs=[
                pl.BlockSpec((half_rows, q_cols), lambda s, h, b: (s, h)),
                pl.BlockSpec((None, half_rows, 1), lambda s, h, b: (s, 0, 0)),
            ]
            + [pl.BlockSpec((half_rows, 2 * kv_feat), lambda s, h, b: (0, 0))] * len(pieces),
            out_specs=pl.BlockSpec((half_rows, q_cols), lambda s, h, b: (s, h)),
            scratch_shapes=[
                pltpu.VMEM((DH, window), kv_slab.dtype),
                pltpu.VMEM((window, 2 * DH), kv_slab.dtype),
            ],
        ),
    )(block_ids, head_queries, starts, *pieces)
    return lax.all_to_all(merged, "kvh", split_axis=0, concat_axis=1, tiled=True)


def solution(mesh):
    return jax.shard_map(
        on_device,
        mesh=mesh,
        in_specs=(P(("seq", "kvh"), None), P(("seq", "kvh"), None), P(("seq", "kvh"), None), P()),
        out_specs=P(("seq", "kvh"), None),
        check_vma=False,
    )
```
